256 devices in a mesh: sens: 64 (over x, z_hi, y), grp: 4 (over z_lo, core).
Axes of the slice: x: 4, y: 4, z: 8 (z_hi: 4, z_lo: 2; z = z_hi * 2 + z_lo), core: 2. Of those that a mesh axis runs over, the one named last changes fastest.
Arguments:
- histories: bfloat16 [2048, 4096], P('sens', 'grp'), may hold values from -6 to 6
- bin_index: int32 [16], replicated, may hold values from 1 to 2047
- delays: int32 [2048, 4096], P('sens'), may hold values from 0 to 4095
- map_adjoint: float32 [4096], replicated, may hold values from -48 to 48
Outputs:
- history_adjoint: bfloat16 [2048, 4096], P('sens', 'grp')
The draws below stay inside these ranges and needn't reach their ends.
Inputs may be any that keep to these rules, and one draw needn't show every extreme that they name: `delays`: each delay is already reduced modulo 4096.
All inputs are finite; a program needn't handle non-finite values.
Results may differ from the reference program's by a relative error of at most 0.0059.
Values may be sent and summed in bfloat16 or wider, within the bound.
No kernel may reach another device: no remote copies, remote signals or barrier semaphores. Data moves between devices by JAX's collectives and lax.ppermute only.
A program may use at most 64 MiB of HBM per device.

```python
import math
import jax
import jax.numpy as jnp
from jax import lax

NT = 4096
F = 16
G = 4096
SENSORS = 2048


def with_ends(entries, stream_key, least, high):
    dims = entries.shape
    spot = [jax.random.randint(jax.random.fold_in(stream_key, axis), (), 0, dims[axis]) for axis in range(len(dims))]
    entries = entries.at[tuple(spot)].set(least)
    longest = dims.index(max(dims))
    spot[longest] = (spot[longest] + 1) % dims[longest]
    return entries.at[tuple(spot)].set(high)


def steps_of(rng, dims, cuts, smallest, high):
    level, own = 1.0, jax.random.fold_in(rng, 6)
    for dim, shards_of in cuts:
        steps = jnp.exp(jax.random.uniform(jax.random.fold_in(own, dim), (shards_of,), jnp.float32, smallest / len(cuts), high / len(cuts)))
        level = level * jnp.repeat(steps, dims[dim] // shards_of).reshape([-1 if axis == dim else 1 for axis in range(len(dims))])
    return level


def centred(stream_key, extent, scale, limit, cuts=(), kind=jnp.bfloat16):
    values = jax.random.normal(stream_key, extent, jnp.float32) * scale
    if len(cuts) > 0:
        values = steps_of(stream_key, extent, cuts, -0.22, 0.18) * values
    return jnp.clip(values, min=-limit, max=limit).astype(kind)


def setup_inputs(seed: int = 0) -> dict:
    streams_of = jax.random.split(jax.random.key(seed), 5)
    histories = centred(streams_of[0], (SENSORS, NT), 1.0, 6.0, ((0, 64), (1, 4)))
    bin_index = with_ends(jax.random.randint(streams_of[1], (F,), 1, NT // 2), jax.random.fold_in(streams_of[1], 1), 1, (NT // 2) - 1).astype(jnp.int32)
    delays = with_ends(jax.random.randint(streams_of[2], (SENSORS, G), 0, NT), jax.random.fold_in(streams_of[2], 1), 0, NT - 1).astype(jnp.int32)
    map_adjoint = centred(streams_of[3], (G,), 8.0, 48.0, (), jnp.float32)
    return {"histories": histories, "bin_index": bin_index, "delays": delays, "map_adjoint": map_adjoint}


two_pi = 2.0 * math.pi

def plain_transform(length, bin_index):
    sample_times = jnp.arange(length, dtype=jnp.int32)
    phase_index = sample_times[:, None] * bin_index[None, :] % length
    phase_angle = phase_index.astype(jnp.float32) * (two_pi / length)
    factor = 1.0 / math.sqrt(length)
    cosine = jnp.cos(phase_angle) * factor
    sine_part = -jnp.sin(phase_angle) * factor
    return jnp.concatenate([cosine, sine_part], 1).astype(jnp.bfloat16)

def angles(bin_index, delay_block, length):
    phase_index = bin_index[:, None, None] * delay_block[None, :, :] % length
    return phase_index.astype(jnp.float32) * (two_pi / length)

def steer_forward(real_part, imag_part, delays, bin_index, length, steer_scale, block_cap):
    scan_count = delays.shape[1]
    block_size = math.gcd(scan_count, block_cap)
    real_trans = real_part.T
    imag_trans = imag_part.T
    highest = lax.Precision.HIGHEST

    def one_block(block_index):
        delay_block = lax.dynamic_slice_in_dim(delays, block_index * block_size, block_size, 1)
        phase_angle = angles(bin_index, delay_block, length)
        cosine = jnp.cos(phase_angle)
        sine_part = jnp.sin(phase_angle)
        steer_real = jnp.einsum('fs,fsg->fg', real_trans, cosine, precision=highest) - jnp.einsum('fs,fsg->fg', imag_trans, sine_part, precision=highest)
        steer_imag = jnp.einsum('fs,fsg->fg', real_trans, sine_part, precision=highest) + jnp.einsum('fs,fsg->fg', imag_trans, cosine, precision=highest)
        return (steer_real * steer_scale, steer_imag * steer_scale)
    blocks_real, blocks_imag = lax.map(one_block, jnp.arange(scan_count // block_size, dtype=jnp.int32))
    bin_count = bin_index.shape[0]
    return (blocks_real.transpose(1, 0, 2).reshape(bin_count, scan_count), blocks_imag.transpose(1, 0, 2).reshape(bin_count, scan_count))

def steer_back(bar_real, bar_imag, delays, bin_index, length, steer_scale, block_cap):
    scan_count = delays.shape[1]
    block_size = math.gcd(scan_count, block_cap)
    highest = lax.Precision.HIGHEST

    def add_block(block_index, totals):
        delay_block = lax.dynamic_slice_in_dim(delays, block_index * block_size, block_size, 1)
        block_real = lax.dynamic_slice_in_dim(bar_real, block_index * block_size, block_size, 1)
        block_imag = lax.dynamic_slice_in_dim(bar_imag, block_index * block_size, block_size, 1)
        phase_angle = angles(bin_index, delay_block, length)
        cosine = jnp.cos(phase_angle)
        sine_part = jnp.sin(phase_angle)
        back_real = jnp.einsum('fg,fsg->fs', block_real, cosine, precision=highest) + jnp.einsum('fg,fsg->fs', block_imag, sine_part, precision=highest)
        back_imag = jnp.einsum('fg,fsg->fs', block_imag, cosine, precision=highest) - jnp.einsum('fg,fsg->fs', block_real, sine_part, precision=highest)
        return (totals[0] + back_real, totals[1] + back_imag)
    zeros_start = jnp.zeros((bin_index.shape[0], delays.shape[0]), jnp.float32)
    total_real, total_imag = lax.fori_loop(0, scan_count // block_size, add_block, (zeros_start, zeros_start))
    return (total_real.T * steer_scale, total_imag.T * steer_scale)

def reference(histories, bin_index, delays, map_adjoint):
    transform = plain_transform(NT, bin_index)
    spectra = jnp.dot(histories, transform, preferred_element_type=jnp.float32)
    real_part = spectra[:, :F]
    imag_part = spectra[:, F:]
    steer_scale = 1.0 / math.sqrt(SENSORS)
    steer_real, steer_imag = steer_forward(real_part, imag_part, delays, bin_index, NT, steer_scale, 32)
    weight = 2.0 * map_adjoint[None, :]
    back_real, back_imag = steer_back(weight * steer_real, weight * steer_imag, delays, bin_index, NT, steer_scale, 32)
    adjoint = jnp.concatenate([back_real, back_imag], 1).astype(jnp.bfloat16)
    return jnp.dot(adjoint, transform.T, preferred_element_type=jnp.float32).astype(jnp.bfloat16)
```

```python
import math

import jax
import jax.numpy as jnp
from jax import lax
from jax.sharding import PartitionSpec as P

NT = 4096

two_pi = 2.0 * math.pi


def transform_rows(first, count, bin_index, length):
    sample_times = first + lax.iota(jnp.int32, count)
    phase_index = sample_times[:, None] * bin_index[None, :] % length
    phase_angle = phase_index.astype(jnp.float32) * (two_pi / length)
    factor = 1.0 / math.sqrt(length)
    cosine = jnp.cos(phase_angle) * factor
    sine_part = -jnp.sin(phase_angle) * factor
    return jnp.concatenate([cosine, sine_part], 1).astype(jnp.bfloat16)


def on_device(histories, bin_index, delays, map_adjoint):
    groups = lax.axis_size("grp")
    position = lax.axis_index("grp")
    bins = bin_index.shape[0]
    sensors = delays.shape[0] * lax.axis_size(SENS_AXES)
    steer_scale = 1.0 / math.sqrt(sensors)
    samples = histories.shape[1]
    scan_share = delays.shape[1] // groups

    transform = transform_rows(position * samples, samples, bin_index, NT)
    spectra = jnp.dot(histories, transform, preferred_element_type=jnp.float32)
    spectra = lax.psum(spectra, "grp")
    real_t = spectra[:, :bins].T
    imag_t = spectra[:, bins:].T

    own_delays = lax.dynamic_slice_in_dim(delays, position * scan_share, scan_share, 1)
    own_weight = 2.0 * lax.dynamic_slice_in_dim(map_adjoint, position * scan_share, scan_share, 0)
    phase_index = (bin_index[:, None, None] * own_delays[None, :, :]) % NT
    phase_angle = phase_index.astype(jnp.float32) * (two_pi / NT)
    cosine = jnp.cos(phase_angle)
    sine_part = jnp.sin(phase_angle)

    steer_real = jnp.sum(real_t[:, :, None] * cosine - imag_t[:, :, None] * sine_part, axis=1)
    steer_imag = jnp.sum(real_t[:, :, None] * sine_part + imag_t[:, :, None] * cosine, axis=1)
    steered = jnp.stack([steer_real, steer_imag]) * steer_scale
    for axis in SENS_AXES[::-1]:
        steered = lax.psum(steered, axis)
    bar_real = own_weight[None, :] * steered[0]
    bar_imag = own_weight[None, :] * steered[1]

    back_real = jnp.sum(bar_real[:, None, :] * cosine + bar_imag[:, None, :] * sine_part, axis=2)
    back_imag = jnp.sum(bar_imag[:, None, :] * cosine - bar_real[:, None, :] * sine_part, axis=2)
    back = jnp.concatenate([back_real.T, back_imag.T], 1) * steer_scale
    back = jnp.sum(lax.all_gather(back, "grp"), axis=0)
    adjoint = back.astype(jnp.bfloat16)
    local_part = lax.dot_general(
        adjoint, transform, (((1,), (1,)), ((), ())), preferred_element_type=jnp.float32
    )
    return local_part.astype(jnp.bfloat16)


SENS_AXES = ("sx", "sz", "sy")


def solution(mesh):
    sens_size = mesh.shape["sens"]
    side = round(sens_size ** (1.0 / 3.0))
    assert side ** 3 == sens_size
    fine = jax.sharding.Mesh(
        mesh.devices.reshape(side, side, side, mesh.shape["grp"]), SENS_AXES + ("grp",)
    )
    placed = (P(SENS_AXES, "grp"), P(), P(SENS_AXES, None), P())
    return jax.shard_map(
        on_device, mesh=fine, in_specs=placed, out_specs=P(SENS_AXES, "grp"), check_vma=False
    )
```

```python
import math

import jax
import jax.numpy as jnp
from jax import lax
from jax.sharding import PartitionSpec as P

NT = 4096

two_pi = 2.0 * math.pi


def transform_rows(first, count, bin_index, length):
    sample_times = first + lax.iota(jnp.int32, count)
    phase_index = sample_times[:, None] * bin_index[None, :] % length
    phase_angle = phase_index.astype(jnp.float32) * (two_pi / length)
    factor = 1.0 / math.sqrt(length)
    cosine = jnp.cos(phase_angle) * factor
    sine_part = -jnp.sin(phase_angle) * factor
    return jnp.concatenate([cosine, sine_part], 1).astype(jnp.bfloat16)


def scatter_sum(x, axis):
    count = lax.axis_size(axis)
    parts = x.reshape(x.shape[:-1] + (count, x.shape[-1] // count))
    parts = jnp.moveaxis(parts, -2, 0)
    return jnp.sum(lax.all_to_all(parts, axis, 0, 0, tiled=True), axis=0)


def gather_last(x, axis):
    count = lax.axis_size(axis)
    copies = jnp.broadcast_to(x[None], (count,) + x.shape)
    joined = jnp.moveaxis(lax.all_to_all(copies, axis, 0, 0, tiled=True), 0, -2)
    return joined.reshape(x.shape[:-1] + (count * x.shape[-1],))


def on_device(histories, bin_index, delays, map_adjoint):
    groups = lax.axis_size("grp")
    position = lax.axis_index("grp")
    bins = bin_index.shape[0]
    sensors = delays.shape[0] * lax.axis_size(SENS_AXES)
    steer_scale = 1.0 / math.sqrt(sensors)
    samples = histories.shape[1]
    scan_share = delays.shape[1] // groups

    transform = transform_rows(position * samples, samples, bin_index, NT)
    spectra = jnp.dot(histories, transform, preferred_element_type=jnp.float32)
    spectra = jnp.sum(lax.all_gather(spectra, "grp"), axis=0)
    real_t = spectra[:, :bins].T
    imag_t = spectra[:, bins:].T

    own_delays = lax.dynamic_slice_in_dim(delays, position * scan_share, scan_share, 1)
    own_weight = 2.0 * lax.dynamic_slice_in_dim(map_adjoint, position * scan_share, scan_share, 0)
    phase_index = (bin_index[:, None, None] * own_delays[None, :, :]) % NT
    phase_angle = phase_index.astype(jnp.float32) * (two_pi / NT)
    cosine = jnp.cos(phase_angle)
    sine_part = jnp.sin(phase_angle)

    steer_real = jnp.sum(real_t[:, :, None] * cosine - imag_t[:, :, None] * sine_part, axis=1)
    steer_imag = jnp.sum(real_t[:, :, None] * sine_part + imag_t[:, :, None] * cosine, axis=1)
    steered = jnp.stack([steer_real, steer_imag]) * steer_scale
    offset = 0
    for axis in SENS_AXES[::-1]:
        steered = scatter_sum(steered, axis)
        offset = offset * lax.axis_size(axis) + lax.axis_index(axis)
    width = steered.shape[-1]
    bar = lax.dynamic_slice_in_dim(own_weight, offset * width, width, 0) * steered
    for axis in SENS_AXES:
        bar = gather_last(bar, axis)
    bar_real = bar[0]
    bar_imag = bar[1]

    back_real = jnp.sum(bar_real[:, None, :] * cosine + bar_imag[:, None, :] * sine_part, axis=2)
    back_imag = jnp.sum(bar_imag[:, None, :] * cosine - bar_real[:, None, :] * sine_part, axis=2)
    back = jnp.concatenate([back_real.T, back_imag.T], 1) * steer_scale
    back = jnp.sum(lax.all_gather(back, "grp"), axis=0)
    adjoint = back.astype(jnp.bfloat16)
    local_part = lax.dot_general(
        adjoint, transform, (((1,), (1,)), ((), ())), preferred_element_type=jnp.float32
    )
    return local_part.astype(jnp.bfloat16)


SENS_AXES = ("sx", "sz", "sy")


def solution(mesh):
    sens_size = mesh.shape["sens"]
    side = round(sens_size ** (1.0 / 3.0))
    assert side ** 3 == sens_size
    fine = jax.sharding.Mesh(
        mesh.devices.reshape(side, side, side, mesh.shape["grp"]), SENS_AXES + ("grp",)
    )
    placed = (P(SENS_AXES, "grp"), P(), P(SENS_AXES, None), P())
    return jax.shard_map(
        on_device, mesh=fine, in_specs=placed, out_specs=P(SENS_AXES, "grp"), check_vma=False
    )
```

```python
import math

import jax
import jax.numpy as jnp
from jax import lax
from jax.sharding import PartitionSpec as P

NT = 4096

two_pi = 2.0 * math.pi


def transform_rows(first, count, bin_index, length):
    sample_times = first + lax.iota(jnp.int32, count)
    phase_index = sample_times[:, None] * bin_index[None, :] % length
    phase_angle = phase_index.astype(jnp.float32) * (two_pi / length)
    factor = 1.0 / math.sqrt(length)
    cosine = jnp.cos(phase_angle) * factor
    sine_part = -jnp.sin(phase_angle) * factor
    return jnp.concatenate([cosine, sine_part], 1).astype(jnp.bfloat16)


def scatter_sum(x, axis):
    count = lax.axis_size(axis)
    lead = x.shape[:-1]
    parts = x.reshape(lead + (count, x.shape[-1] // count))
    parts = jnp.moveaxis(parts, -2, 0).reshape(count, -1)
    total = jnp.sum(lax.all_to_all(parts, axis, 0, 0, tiled=True), axis=0)
    return total.reshape(lead + (x.shape[-1] // count,))


def gather_last(x, axis):
    count = lax.axis_size(axis)
    copies = jnp.broadcast_to(x.reshape(1, -1), (count, x.size))
    joined = lax.all_to_all(copies, axis, 0, 0, tiled=True).reshape((count,) + x.shape)
    joined = jnp.moveaxis(joined, 0, -2)
    return joined.reshape(x.shape[:-1] + (count * x.shape[-1],))


def on_device(histories, bin_index, delays, map_adjoint):
    groups = lax.axis_size("grp")
    position = lax.axis_index("grp")
    bins = bin_index.shape[0]
    sensors = delays.shape[0] * lax.axis_size(SENS_AXES)
    steer_scale = 1.0 / math.sqrt(sensors)
    samples = histories.shape[1]
    scan_share = delays.shape[1] // groups

    transform = transform_rows(position * samples, samples, bin_index, NT)
    spectra = jnp.dot(histories, transform, preferred_element_type=jnp.float32)
    spectra = jnp.sum(lax.all_gather(spectra, "grp"), axis=0)
    real_t = spectra[:, :bins].T
    imag_t = spectra[:, bins:].T

    own_delays = lax.dynamic_slice_in_dim(delays, position * scan_share, scan_share, 1)
    own_weight = 2.0 * lax.dynamic_slice_in_dim(map_adjoint, position * scan_share, scan_share, 0)
    phase_index = (bin_index[:, None, None] * own_delays[None, :, :]) % NT
    phase_angle = phase_index.astype(jnp.float32) * (two_pi / NT)
    cosine = jnp.cos(phase_angle)
    sine_part = jnp.sin(phase_angle)

    steer_real = jnp.sum(real_t[:, :, None] * cosine - imag_t[:, :, None] * sine_part, axis=1)
    steer_imag = jnp.sum(real_t[:, :, None] * sine_part + imag_t[:, :, None] * cosine, axis=1)
    steered = jnp.stack([steer_real, steer_imag]) * steer_scale
    offset = 0
    for axis in SENS_AXES:
        offset = offset * lax.axis_size(axis) + lax.axis_index(axis)
    steered = scatter_sum(steered, SENS_AXES)
    width = steered.shape[-1]
    bar = lax.dynamic_slice_in_dim(own_weight, offset * width, width, 0) * steered
    bar = gather_last(bar, SENS_AXES)
    bar_real = bar[0]
    bar_imag = bar[1]

    back_real = jnp.sum(bar_real[:, None, :] * cosine + bar_imag[:, None, :] * sine_part, axis=2)
    back_imag = jnp.sum(bar_imag[:, None, :] * cosine - bar_real[:, None, :] * sine_part, axis=2)
    back = jnp.concatenate([back_real.T, back_imag.T], 1) * steer_scale
    back = jnp.sum(lax.all_gather(back, "grp"), axis=0)
    adjoint = back.astype(jnp.bfloat16)
    local_part = lax.dot_general(
        adjoint, transform, (((1,), (1,)), ((), ())), preferred_element_type=jnp.float32
    )
    return local_part.astype(jnp.bfloat16)


SENS_AXES = ("sx", "sz", "sy")


def solution(mesh):
    sens_size = mesh.shape["sens"]
    side = round(sens_size ** (1.0 / 3.0))
    assert side ** 3 == sens_size
    fine = jax.sharding.Mesh(
        mesh.devices.reshape(side, side, side, mesh.shape["grp"]), SENS_AXES + ("grp",)
    )
    placed = (P(SENS_AXES, "grp"), P(), P(SENS_AXES, None), P())
    return jax.shard_map(
        on_device, mesh=fine, in_specs=placed, out_specs=P(SENS_AXES, "grp"), check_vma=False
    )
```

```python
import math

import jax
import jax.numpy as jnp
from jax import lax
from jax.sharding import PartitionSpec as P

NT = 4096

two_pi = 2.0 * math.pi


def transform_rows(first, count, bin_index, length):
    sample_times = first + lax.iota(jnp.int32, count)
    phase_index = sample_times[:, None] * bin_index[None, :] % length
    phase_angle = phase_index.astype(jnp.float32) * (two_pi / length)
    factor = 1.0 / math.sqrt(length)
    cosine = jnp.cos(phase_angle) * factor
    sine_part = -jnp.sin(phase_angle) * factor
    return jnp.concatenate([cosine, sine_part], 1).astype(jnp.bfloat16)


def shifted(x, axis, shift):
    count = lax.axis_size(axis)
    return lax.ppermute(x, axis, [(j, (j + shift) % count) for j in range(count)])


def scatter_sum(x, axis):
    count = lax.axis_size(axis)
    me = lax.axis_index(axis)
    lead = x.shape[:-1]
    width = x.shape[-1] // count
    parts = jnp.moveaxis(x.reshape(lead + (count, width)), -2, 0)
    total = parts[me]
    for shift in range(1, count):
        total = total + shifted(parts[(me + shift) % count], axis, shift)
    return total


def gather_stack(x, axis):
    count = lax.axis_size(axis)
    me = lax.axis_index(axis)
    stack = jnp.stack([x] + [shifted(x, axis, shift) for shift in range(1, count)])
    return stack[(me - jnp.arange(count)) % count]


def gather_last(x, axis):
    joined = jnp.moveaxis(gather_stack(x, axis), 0, -2)
    return joined.reshape(x.shape[:-1] + (joined.shape[-2] * x.shape[-1],))


def on_device(histories, bin_index, delays, map_adjoint):
    groups = lax.axis_size("grp")
    position = lax.axis_index("grp")
    bins = bin_index.shape[0]
    sensors = delays.shape[0] * lax.axis_size(SENS_AXES)
    steer_scale = 1.0 / math.sqrt(sensors)
    samples = histories.shape[1]
    scan_share = delays.shape[1] // groups

    transform = transform_rows(position * samples, samples, bin_index, NT)
    spectra = jnp.dot(histories, transform, preferred_element_type=jnp.float32)
    spectra = jnp.sum(gather_stack(spectra, "grp"), axis=0)
    real_t = spectra[:, :bins].T
    imag_t = spectra[:, bins:].T

    own_delays = lax.dynamic_slice_in_dim(delays, position * scan_share, scan_share, 1)
    own_weight = 2.0 * lax.dynamic_slice_in_dim(map_adjoint, position * scan_share, scan_share, 0)
    phase_index = (bin_index[:, None, None] * own_delays[None, :, :]) % NT
    phase_angle = phase_index.astype(jnp.float32) * (two_pi / NT)
    cosine = jnp.cos(phase_angle)
    sine_part = jnp.sin(phase_angle)

    steer_real = jnp.sum(real_t[:, :, None] * cosine - imag_t[:, :, None] * sine_part, axis=1)
    steer_imag = jnp.sum(real_t[:, :, None] * sine_part + imag_t[:, :, None] * cosine, axis=1)
    steered = jnp.stack([steer_real, steer_imag]) * steer_scale
    offset = 0
    for axis in REDUCE_ORDER:
        steered = scatter_sum(steered, axis)
        offset = offset * lax.axis_size(axis) + lax.axis_index(axis)
    width = steered.shape[-1]
    bar = lax.dynamic_slice_in_dim(own_weight, offset * width, width, 0) * steered
    for axis in REDUCE_ORDER[::-1]:
        bar = gather_last(bar, axis)
    bar_real = bar[0]
    bar_imag = bar[1]

    back_real = jnp.sum(bar_real[:, None, :] * cosine + bar_imag[:, None, :] * sine_part, axis=2)
    back_imag = jnp.sum(bar_imag[:, None, :] * cosine - bar_real[:, None, :] * sine_part, axis=2)
    back = jnp.concatenate([back_real.T, back_imag.T], 1) * steer_scale
    back = jnp.sum(gather_stack(back, "grp"), axis=0)
    adjoint = back.astype(jnp.bfloat16)
    local_part = lax.dot_general(
        adjoint, transform, (((1,), (1,)), ((), ())), preferred_element_type=jnp.float32
    )
    return local_part.astype(jnp.bfloat16)


SENS_AXES = ("sx", "sz", "sy")
REDUCE_ORDER = ("sy", "sx", "sz")


def solution(mesh):
    sens_size = mesh.shape["sens"]
    side = round(sens_size ** (1.0 / 3.0))
    assert side ** 3 == sens_size
    fine = jax.sharding.Mesh(
        mesh.devices.reshape(side, side, side, mesh.shape["grp"]), SENS_AXES + ("grp",)
    )
    placed = (P(SENS_AXES, "grp"), P(), P(SENS_AXES, None), P())
    return jax.shard_map(
        on_device, mesh=fine, in_specs=placed, out_specs=P(SENS_AXES, "grp"), check_vma=False
    )
```

```python
import math

import jax
import jax.numpy as jnp
from jax import lax
from jax.sharding import PartitionSpec as P

NT = 4096

two_pi = 2.0 * math.pi


def transform_rows(first, count, bin_index, length):
    sample_times = first + lax.iota(jnp.int32, count)
    phase_index = sample_times[:, None] * bin_index[None, :] % length
    phase_angle = phase_index.astype(jnp.float32) * (two_pi / length)
    factor = 1.0 / math.sqrt(length)
    cosine = jnp.cos(phase_angle) * factor
    sine_part = -jnp.sin(phase_angle) * factor
    return jnp.concatenate([cosine, sine_part], 1).astype(jnp.bfloat16)


def circle_point(phase_index, length):
    quarter = length // 4
    eighth = length // 8
    quadrant = phase_index // quarter
    rest = phase_index - quadrant * quarter
    flip = rest > eighth
    folded = jnp.where(flip, quarter - rest, rest)
    x = folded.astype(jnp.float32) * (two_pi / length)
    x2 = x * x
    sin_x = x * (1.0 + x2 * (-1.0 / 6.0 + x2 * (1.0 / 120.0 + x2 * (-1.0 / 5040.0))))
    cos_x = 1.0 + x2 * (-0.5 + x2 * (1.0 / 24.0 + x2 * (-1.0 / 720.0 + x2 * (1.0 / 40320.0))))
    sin_r = jnp.where(flip, cos_x, sin_x)
    cos_r = jnp.where(flip, sin_x, cos_x)
    sine = jnp.where(quadrant == 0, sin_r, jnp.where(quadrant == 1, cos_r, jnp.where(quadrant == 2, -sin_r, -cos_r)))
    cosine = jnp.where(quadrant == 0, cos_r, jnp.where(quadrant == 1, -sin_r, jnp.where(quadrant == 2, -cos_r, sin_r)))
    return cosine, sine


def shifted(x, axis, shift):
    count = lax.axis_size(axis)
    return lax.ppermute(x, axis, [(j, (j + shift) % count) for j in range(count)])


def gather_stack(x, axis):
    count = lax.axis_size(axis)
    me = lax.axis_index(axis)
    stack = jnp.stack([x] + [shifted(x, axis, shift) for shift in range(1, count)])
    return stack[(me - jnp.arange(count)) % count]


def scatter_sum(x, axis):
    count = lax.axis_size(axis)
    lead = x.shape[:-1]
    parts = x.reshape(lead + (count, x.shape[-1] // count))
    parts = jnp.moveaxis(parts, -2, 0).reshape(count, -1)
    total = jnp.sum(lax.all_to_all(parts, axis, 0, 0, tiled=True), axis=0)
    return total.reshape(lead + (x.shape[-1] // count,))


def gather_last(x, axis):
    count = lax.axis_size(axis)
    copies = jnp.broadcast_to(x.reshape(1, -1), (count, x.size))
    joined = lax.all_to_all(copies, axis, 0, 0, tiled=True).reshape((count,) + x.shape)
    joined = jnp.moveaxis(joined, 0, -2)
    return joined.reshape(x.shape[:-1] + (count * x.shape[-1],))


def on_device(histories, bin_index, delays, map_adjoint):
    groups = lax.axis_size("grp")
    position = lax.axis_index("grp")
    bins = bin_index.shape[0]
    sensors = delays.shape[0] * lax.axis_size(SENS_AXES)
    steer_scale = 1.0 / math.sqrt(sensors)
    samples = histories.shape[1]
    scan_share = delays.shape[1] // groups

    transform = transform_rows(position * samples, samples, bin_index, NT)
    spectra = jnp.dot(histories, transform, preferred_element_type=jnp.float32)
    spectra = jnp.sum(gather_stack(spectra, "grp"), axis=0)
    real_t = spectra[:, :bins].T
    imag_t = spectra[:, bins:].T

    own_delays = lax.dynamic_slice_in_dim(delays, position * scan_share, scan_share, 1)
    own_weight = 2.0 * lax.dynamic_slice_in_dim(map_adjoint, position * scan_share, scan_share, 0)
    phase_index = (bin_index[:, None, None] * own_delays[None, :, :]) % NT
    cosine, sine_part = lax.optimization_barrier(circle_point(phase_index, NT))

    steer_real = jnp.sum(real_t[:, :, None] * cosine - imag_t[:, :, None] * sine_part, axis=1)
    steer_imag = jnp.sum(real_t[:, :, None] * sine_part + imag_t[:, :, None] * cosine, axis=1)
    steered = jnp.stack([steer_real, steer_imag]) * steer_scale
    offset = 0
    for axis in SENS_AXES:
        offset = offset * lax.axis_size(axis) + lax.axis_index(axis)
    steered = scatter_sum(steered, SENS_AXES)
    width = steered.shape[-1]
    bar = lax.dynamic_slice_in_dim(own_weight, offset * width, width, 0) * steered
    bar = gather_last(bar, SENS_AXES)
    bar_real = bar[0]
    bar_imag = bar[1]

    back_real = jnp.sum(bar_real[:, None, :] * cosine + bar_imag[:, None, :] * sine_part, axis=2)
    back_imag = jnp.sum(bar_imag[:, None, :] * cosine - bar_real[:, None, :] * sine_part, axis=2)
    back = jnp.concatenate([back_real.T, back_imag.T], 1) * steer_scale
    back = jnp.sum(gather_stack(back, "grp"), axis=0)
    adjoint = back.astype(jnp.bfloat16)
    local_part = lax.dot_general(
        adjoint, transform, (((1,), (1,)), ((), ())), preferred_element_type=jnp.float32
    )
    return local_part.astype(jnp.bfloat16)


SENS_AXES = ("sx", "sz", "sy")


def solution(mesh):
    sens_size = mesh.shape["sens"]
    side = round(sens_size ** (1.0 / 3.0))
    assert side ** 3 == sens_size
    fine = jax.sharding.Mesh(
        mesh.devices.reshape(side, side, side, mesh.shape["grp"]), SENS_AXES + ("grp",)
    )
    placed = (P(SENS_AXES, "grp"), P(), P(SENS_AXES, None), P())
    return jax.shard_map(
        on_device, mesh=fine, in_specs=placed, out_specs=P(SENS_AXES, "grp"), check_vma=False
    )
```

```python
import math

import jax
import jax.numpy as jnp
from jax import lax
from jax.sharding import PartitionSpec as P

NT = 4096

two_pi = 2.0 * math.pi


def transform_rows(first, count, bin_index, length):
    sample_times = first + lax.iota(jnp.int32, count)
    phase_index = sample_times[:, None] * bin_index[None, :] % length
    phase_angle = phase_index.astype(jnp.float32) * (two_pi / length)
    factor = 1.0 / math.sqrt(length)
    cosine = jnp.cos(phase_angle) * factor
    sine_part = -jnp.sin(phase_angle) * factor
    return jnp.concatenate([cosine, sine_part], 1).astype(jnp.bfloat16)


def circle_point(phase_index, length):
    quarter = length // 4
    eighth = length // 8
    quadrant = phase_index // quarter
    rest = phase_index - quadrant * quarter
    flip = rest > eighth
    folded = jnp.where(flip, quarter - rest, rest)
    x = folded.astype(jnp.float32) * (two_pi / length)
    x2 = x * x
    sin_x = x * (1.0 + x2 * (-1.0 / 6.0 + x2 * (1.0 / 120.0 + x2 * (-1.0 / 5040.0))))
    cos_x = 1.0 + x2 * (-0.5 + x2 * (1.0 / 24.0 + x2 * (-1.0 / 720.0 + x2 * (1.0 / 40320.0))))
    sin_r = jnp.where(flip, cos_x, sin_x)
    cos_r = jnp.where(flip, sin_x, cos_x)
    sine = jnp.where(quadrant == 0, sin_r, jnp.where(quadrant == 1, cos_r, jnp.where(quadrant == 2, -sin_r, -cos_r)))
    cosine = jnp.where(quadrant == 0, cos_r, jnp.where(quadrant == 1, -sin_r, jnp.where(quadrant == 2, -cos_r, sin_r)))
    return cosine, sine


def shifted(x, axis, shift):
    count = lax.axis_size(axis)
    return lax.ppermute(x, axis, [(j, (j + shift) % count) for j in range(count)])


def gather_stack(x, axis):
    count = lax.axis_size(axis)
    me = lax.axis_index(axis)
    stack = jnp.stack([x] + [shifted(x, axis, shift) for shift in range(1, count)])
    return stack[(me - jnp.arange(count)) % count]


def scatter_sum(x, axis):
    count = lax.axis_size(axis)
    lead = x.shape[:-1]
    parts = x.reshape(lead + (count, x.shape[-1] // count))
    parts = jnp.moveaxis(parts, -2, 0).reshape(count, -1)
    moved = lax.all_to_all(parts.astype(jnp.bfloat16), axis, 0, 0, tiled=True)
    total = jnp.sum(moved.astype(jnp.float32), axis=0)
    return total.reshape(lead + (x.shape[-1] // count,))


def gather_last(x, axis):
    count = lax.axis_size(axis)
    copies = jnp.broadcast_to(x.reshape(1, -1).astype(jnp.bfloat16), (count, x.size))
    joined = lax.all_to_all(copies, axis, 0, 0, tiled=True).astype(jnp.float32)
    joined = joined.reshape((count,) + x.shape)
    joined = jnp.moveaxis(joined, 0, -2)
    return joined.reshape(x.shape[:-1] + (count * x.shape[-1],))


def on_device(histories, bin_index, delays, map_adjoint):
    groups = lax.axis_size("grp")
    position = lax.axis_index("grp")
    bins = bin_index.shape[0]
    sensors = delays.shape[0] * lax.axis_size(SENS_AXES)
    steer_scale = 1.0 / math.sqrt(sensors)
    samples = histories.shape[1]
    scan_share = delays.shape[1] // groups

    transform = transform_rows(position * samples, samples, bin_index, NT)
    spectra = jnp.dot(histories, transform, preferred_element_type=jnp.float32)
    spectra = jnp.sum(gather_stack(spectra, "grp"), axis=0)
    real_t = spectra[:, :bins].T
    imag_t = spectra[:, bins:].T

    own_delays = lax.dynamic_slice_in_dim(delays, position * scan_share, scan_share, 1)
    own_weight = 2.0 * lax.dynamic_slice_in_dim(map_adjoint, position * scan_share, scan_share, 0)
    phase_index = (bin_index[:, None, None] * own_delays[None, :, :]) % NT
    cosine, sine_part = lax.optimization_barrier(circle_point(phase_index, NT))

    steer_real = jnp.sum(real_t[:, :, None] * cosine - imag_t[:, :, None] * sine_part, axis=1)
    steer_imag = jnp.sum(real_t[:, :, None] * sine_part + imag_t[:, :, None] * cosine, axis=1)
    steered = jnp.stack([steer_real, steer_imag]) * steer_scale
    offset = 0
    for axis in SENS_AXES:
        offset = offset * lax.axis_size(axis) + lax.axis_index(axis)
    steered = scatter_sum(steered, SENS_AXES)
    width = steered.shape[-1]
    bar = lax.dynamic_slice_in_dim(own_weight, offset * width, width, 0) * steered
    bar = gather_last(bar, SENS_AXES)
    bar_real = bar[0]
    bar_imag = bar[1]

    back_real = jnp.sum(bar_real[:, None, :] * cosine + bar_imag[:, None, :] * sine_part, axis=2)
    back_imag = jnp.sum(bar_imag[:, None, :] * cosine - bar_real[:, None, :] * sine_part, axis=2)
    back = jnp.concatenate([back_real.T, back_imag.T], 1) * steer_scale
    back = jnp.sum(gather_stack(back, "grp"), axis=0)
    adjoint = back.astype(jnp.bfloat16)
    local_part = lax.dot_general(
        adjoint, transform, (((1,), (1,)), ((), ())), preferred_element_type=jnp.float32
    )
    return local_part.astype(jnp.bfloat16)


SENS_AXES = ("sx", "sz", "sy")


def solution(mesh):
    sens_size = mesh.shape["sens"]
    side = round(sens_size ** (1.0 / 3.0))
    assert side ** 3 == sens_size
    fine = jax.sharding.Mesh(
        mesh.devices.reshape(side, side, side, mesh.shape["grp"]), SENS_AXES + ("grp",)
    )
    placed = (P(SENS_AXES, "grp"), P(), P(SENS_AXES, None), P())
    return jax.shard_map(
        on_device, mesh=fine, in_specs=placed, out_specs=P(SENS_AXES, "grp"), check_vma=False
    )
```

```python
import math

import jax
import jax.numpy as jnp
from jax import lax
from jax.sharding import PartitionSpec as P

NT = 4096

two_pi = 2.0 * math.pi


def transform_rows(first, count, bin_index, length):
    sample_times = first + lax.iota(jnp.int32, count)
    phase_index = sample_times[:, None] * bin_index[None, :] % length
    phase_angle = phase_index.astype(jnp.float32) * (two_pi / length)
    factor = 1.0 / math.sqrt(length)
    cosine = jnp.cos(phase_angle) * factor
    sine_part = -jnp.sin(phase_angle) * factor
    return jnp.concatenate([cosine, sine_part], 1).astype(jnp.bfloat16)


def circle_point(phase_index, length):
    quarter = length // 4
    eighth = length // 8
    quadrant = phase_index // quarter
    rest = phase_index - quadrant * quarter
    flip = rest > eighth
    folded = jnp.where(flip, quarter - rest, rest)
    x = folded.astype(jnp.float32) * (two_pi / length)
    x2 = x * x
    sin_x = x * (1.0 + x2 * (-1.0 / 6.0 + x2 * (1.0 / 120.0 + x2 * (-1.0 / 5040.0))))
    cos_x = 1.0 + x2 * (-0.5 + x2 * (1.0 / 24.0 + x2 * (-1.0 / 720.0 + x2 * (1.0 / 40320.0))))
    sin_r = jnp.where(flip, cos_x, sin_x)
    cos_r = jnp.where(flip, sin_x, cos_x)
    sine = jnp.where(quadrant == 0, sin_r, jnp.where(quadrant == 1, cos_r, jnp.where(quadrant == 2, -sin_r, -cos_r)))
    cosine = jnp.where(quadrant == 0, cos_r, jnp.where(quadrant == 1, -sin_r, jnp.where(quadrant == 2, -cos_r, sin_r)))
    return cosine, sine


def shifted(x, axis, shift):
    count = lax.axis_size(axis)
    return lax.ppermute(x, axis, [(j, (j + shift) % count) for j in range(count)])


def gather_stack(x, axis):
    count = lax.axis_size(axis)
    me = lax.axis_index(axis)
    stack = jnp.stack([x] + [shifted(x, axis, shift) for shift in range(1, count)])
    return stack[(me - jnp.arange(count)) % count]


def scatter_sum(x, axis):
    count = lax.axis_size(axis)
    lead = x.shape[:-1]
    parts = x.reshape(lead + (count, x.shape[-1] // count))
    parts = jnp.moveaxis(parts, -2, 0).reshape(count, -1)
    total = jnp.sum(lax.all_to_all(parts, axis, 0, 0, tiled=True), axis=0)
    return total.reshape(lead + (x.shape[-1] // count,))


def gather_last(x, axis):
    count = lax.axis_size(axis)
    copies = jnp.broadcast_to(x.reshape(1, -1), (count, x.size))
    joined = lax.all_to_all(copies, axis, 0, 0, tiled=True).reshape((count,) + x.shape)
    joined = jnp.moveaxis(joined, 0, -2)
    return joined.reshape(x.shape[:-1] + (count * x.shape[-1],))


def on_device(histories, bin_index, delays, map_adjoint):
    groups = lax.axis_size("grp")
    position = lax.axis_index("grp")
    bins = bin_index.shape[0]
    sensors = delays.shape[0] * lax.axis_size(SENS_AXES)
    steer_scale = 1.0 / math.sqrt(sensors)
    samples = histories.shape[1]
    scan_share = delays.shape[1] // groups

    transform = transform_rows(position * samples, samples, bin_index, NT)
    spectra = jnp.dot(histories, transform, preferred_element_type=jnp.float32)
    spectra = jnp.sum(gather_stack(spectra, "grp"), axis=0)
    real_t = spectra[:, :bins].T
    imag_t = spectra[:, bins:].T

    own_delays = lax.dynamic_slice_in_dim(delays, position * scan_share, scan_share, 1)
    own_weight = 2.0 * lax.dynamic_slice_in_dim(map_adjoint, position * scan_share, scan_share, 0)
    phase_index = (bin_index[:, None, None] * own_delays[None, :, :]) % NT
    cosine, sine_part = lax.optimization_barrier(circle_point(phase_index, NT))

    steer_real = jnp.sum(real_t[:, :, None] * cosine - imag_t[:, :, None] * sine_part, axis=1)
    steer_imag = jnp.sum(real_t[:, :, None] * sine_part + imag_t[:, :, None] * cosine, axis=1)
    steered = jnp.stack([steer_real, steer_imag]) * steer_scale
    offset = 0
    for axes in REDUCE_GROUPS:
        steered = scatter_sum(steered, axes)
        for axis in axes:
            offset = offset * lax.axis_size(axis) + lax.axis_index(axis)
    width = steered.shape[-1]
    bar = lax.dynamic_slice_in_dim(own_weight, offset * width, width, 0) * steered
    for axes in REDUCE_GROUPS[::-1]:
        bar = gather_last(bar, axes)
    bar_real = bar[0]
    bar_imag = bar[1]

    back_real = jnp.sum(bar_real[:, None, :] * cosine + bar_imag[:, None, :] * sine_part, axis=2)
    back_imag = jnp.sum(bar_imag[:, None, :] * cosine - bar_real[:, None, :] * sine_part, axis=2)
    back = jnp.concatenate([back_real.T, back_imag.T], 1) * steer_scale
    back = jnp.sum(gather_stack(back, "grp"), axis=0)
    adjoint = back.astype(jnp.bfloat16)
    local_part = lax.dot_general(
        adjoint, transform, (((1,), (1,)), ((), ())), preferred_element_type=jnp.float32
    )
    return local_part.astype(jnp.bfloat16)


SENS_AXES = ("sx", "sz", "sy")
REDUCE_GROUPS = (("sx", "sy"), ("sz",))


def solution(mesh):
    sens_size = mesh.shape["sens"]
    side = round(sens_size ** (1.0 / 3.0))
    assert side ** 3 == sens_size
    fine = jax.sharding.Mesh(
        mesh.devices.reshape(side, side, side, mesh.shape["grp"]), SENS_AXES + ("grp",)
    )
    placed = (P(SENS_AXES, "grp"), P(), P(SENS_AXES, None), P())
    return jax.shard_map(
        on_device, mesh=fine, in_specs=placed, out_specs=P(SENS_AXES, "grp"), check_vma=False
    )
```

```python
import math

import jax
import jax.numpy as jnp
from jax import lax
from jax.sharding import PartitionSpec as P

NT = 4096

two_pi = 2.0 * math.pi


def transform_rows(first, count, bin_index, length):
    sample_times = first + lax.iota(jnp.int32, count)
    phase_index = sample_times[:, None] * bin_index[None, :] % length
    phase_angle = phase_index.astype(jnp.float32) * (two_pi / length)
    factor = 1.0 / math.sqrt(length)
    cosine = jnp.cos(phase_angle) * factor
    sine_part = -jnp.sin(phase_angle) * factor
    return jnp.concatenate([cosine, sine_part], 1).astype(jnp.bfloat16)


def circle_point(phase_index, length):
    eighth_bits = (length // 8).bit_length() - 1
    quarter = length // 4
    quadrant = phase_index >> (eighth_bits + 1)
    rest = phase_index & (quarter - 1)
    flip = (rest >> eighth_bits) & (rest != (length // 8)).astype(jnp.int32)
    folded = jnp.where(flip == 1, quarter - rest, rest)
    x = folded.astype(jnp.float32) * (two_pi / length)
    x2 = x * x
    sin_x = x * (1.0 + x2 * (-1.0 / 6.0 + x2 * (1.0 / 120.0 + x2 * (-1.0 / 5040.0))))
    cos_x = 1.0 + x2 * (-0.5 + x2 * (1.0 / 24.0 + x2 * (-1.0 / 720.0 + x2 * (1.0 / 40320.0))))
    swap = ((quadrant & 1) ^ flip) == 1
    sine = jnp.where(swap, cos_x, sin_x)
    cosine = jnp.where(swap, sin_x, cos_x)
    sine = jnp.where(quadrant >= 2, -sine, sine)
    cosine = jnp.where(((quadrant ^ (quadrant >> 1)) & 1) == 1, -cosine, cosine)
    return cosine, sine


def shifted(x, axis, shift):
    count = lax.axis_size(axis)
    return lax.ppermute(x, axis, [(j, (j + shift) % count) for j in range(count)])


def gather_stack(x, axis):
    count = lax.axis_size(axis)
    me = lax.axis_index(axis)
    stack = jnp.stack([x] + [shifted(x, axis, shift) for shift in range(1, count)])
    return stack[(me - jnp.arange(count)) % count]


def scatter_sum(x, axis):
    count = lax.axis_size(axis)
    lead = x.shape[:-1]
    parts = x.reshape(lead + (count, x.shape[-1] // count))
    parts = jnp.moveaxis(parts, -2, 0).reshape(count, -1)
    total = jnp.sum(lax.all_to_all(parts, axis, 0, 0, tiled=True), axis=0)
    return total.reshape(lead + (x.shape[-1] // count,))


def gather_last(x, axis):
    count = lax.axis_size(axis)
    copies = jnp.broadcast_to(x.reshape(1, -1), (count, x.size))
    joined = lax.all_to_all(copies, axis, 0, 0, tiled=True).reshape((count,) + x.shape)
    joined = jnp.moveaxis(joined, 0, -2)
    return joined.reshape(x.shape[:-1] + (count * x.shape[-1],))


def on_device(histories, bin_index, delays, map_adjoint):
    groups = lax.axis_size("grp")
    position = lax.axis_index("grp")
    bins = bin_index.shape[0]
    sensors = delays.shape[0] * lax.axis_size(SENS_AXES)
    steer_scale = 1.0 / math.sqrt(sensors)
    samples = histories.shape[1]
    scan_share = delays.shape[1] // groups

    transform = transform_rows(position * samples, samples, bin_index, NT)
    spectra = jnp.dot(histories, transform, preferred_element_type=jnp.float32)
    spectra = jnp.sum(gather_stack(spectra, "grp"), axis=0)
    real_t = spectra[:, :bins].T
    imag_t = spectra[:, bins:].T

    own_delays = lax.dynamic_slice_in_dim(delays, position * scan_share, scan_share, 1)
    own_weight = 2.0 * lax.dynamic_slice_in_dim(map_adjoint, position * scan_share, scan_share, 0)
    phase_index = (bin_index[:, None, None] * own_delays[None, :, :]) & (NT - 1)
    cosine, sine_part = lax.optimization_barrier(circle_point(phase_index, NT))

    steer_real = jnp.sum(real_t[:, :, None] * cosine - imag_t[:, :, None] * sine_part, axis=1)
    steer_imag = jnp.sum(real_t[:, :, None] * sine_part + imag_t[:, :, None] * cosine, axis=1)
    steered = jnp.stack([steer_real, steer_imag]) * steer_scale
    offset = 0
    for axis in SENS_AXES:
        offset = offset * lax.axis_size(axis) + lax.axis_index(axis)
    steered = scatter_sum(steered, SENS_AXES)
    width = steered.shape[-1]
    bar = lax.dynamic_slice_in_dim(own_weight, offset * width, width, 0) * steered
    bar = gather_last(bar, SENS_AXES)
    bar_real = bar[0]
    bar_imag = bar[1]

    back_real = jnp.sum(bar_real[:, None, :] * cosine + bar_imag[:, None, :] * sine_part, axis=2)
    back_imag = jnp.sum(bar_imag[:, None, :] * cosine - bar_real[:, None, :] * sine_part, axis=2)
    back = jnp.concatenate([back_real.T, back_imag.T], 1) * steer_scale
    back = jnp.sum(gather_stack(back, "grp"), axis=0)
    adjoint = back.astype(jnp.bfloat16)
    local_part = lax.dot_general(
        adjoint, transform, (((1,), (1,)), ((), ())), preferred_element_type=jnp.float32
    )
    return local_part.astype(jnp.bfloat16)


SENS_AXES = ("sx", "sz", "sy")


def solution(mesh):
    sens_size = mesh.shape["sens"]
    side = round(sens_size ** (1.0 / 3.0))
    assert side ** 3 == sens_size
    fine = jax.sharding.Mesh(
        mesh.devices.reshape(side, side, side, mesh.shape["grp"]), SENS_AXES + ("grp",)
    )
    placed = (P(SENS_AXES, "grp"), P(), P(SENS_AXES, None), P())
    return jax.shard_map(
        on_device, mesh=fine, in_specs=placed, out_specs=P(SENS_AXES, "grp"), check_vma=False
    )
```

```python
import math

import jax
import jax.numpy as jnp
from jax import lax
from jax.sharding import PartitionSpec as P

NT = 4096

two_pi = 2.0 * math.pi


def transform_rows(first, count, bin_index, length):
    sample_times = first + lax.iota(jnp.int32, count)
    phase_index = sample_times[:, None] * bin_index[None, :] % length
    phase_angle = phase_index.astype(jnp.float32) * (two_pi / length)
    factor = 1.0 / math.sqrt(length)
    cosine = jnp.cos(phase_angle) * factor
    sine_part = -jnp.sin(phase_angle) * factor
    return jnp.concatenate([cosine, sine_part], 1).astype(jnp.bfloat16)


def circle_point(phase_index, length):
    eighth_bits = (length // 8).bit_length() - 1
    quarter = length // 4
    quadrant = phase_index >> (eighth_bits + 1)
    rest = phase_index & (quarter - 1)
    flip = (rest >> eighth_bits) & (rest != (length // 8)).astype(jnp.int32)
    folded = jnp.where(flip == 1, quarter - rest, rest)
    x = folded.astype(jnp.float32) * (two_pi / length)
    x2 = x * x
    sin_x = x * (1.0 + x2 * (-1.0 / 6.0 + x2 * (1.0 / 120.0 + x2 * (-1.0 / 5040.0))))
    cos_x = 1.0 + x2 * (-0.5 + x2 * (1.0 / 24.0 + x2 * (-1.0 / 720.0 + x2 * (1.0 / 40320.0))))
    swap = ((quadrant & 1) ^ flip) == 1
    sine = jnp.where(swap, cos_x, sin_x)
    cosine = jnp.where(swap, sin_x, cos_x)
    sine = jnp.where(quadrant >= 2, -sine, sine)
    cosine = jnp.where(((quadrant ^ (quadrant >> 1)) & 1) == 1, -cosine, cosine)
    return cosine, sine


def shifted(x, axis, shift):
    count = lax.axis_size(axis)
    return lax.ppermute(x, axis, [(j, (j + shift) % count) for j in range(count)])


def gather_stack(x, axis):
    count = lax.axis_size(axis)
    me = lax.axis_index(axis)
    stack = jnp.stack([x] + [shifted(x, axis, shift) for shift in range(1, count)])
    return stack[(me - jnp.arange(count)) % count]


def scatter_sum(x, axis):
    count = lax.axis_size(axis)
    lead = x.shape[:-1]
    parts = x.reshape(lead + (count, x.shape[-1] // count))
    parts = jnp.moveaxis(parts, -2, 0).reshape(count, -1)
    total = jnp.sum(lax.all_to_all(parts, axis, 0, 0, tiled=True), axis=0)
    return total.reshape(lead + (x.shape[-1] // count,))


def gather_last(x, axis):
    count = lax.axis_size(axis)
    copies = jnp.broadcast_to(x.reshape(1, -1), (count, x.size))
    joined = lax.all_to_all(copies, axis, 0, 0, tiled=True).reshape((count,) + x.shape)
    joined = jnp.moveaxis(joined, 0, -2)
    return joined.reshape(x.shape[:-1] + (count * x.shape[-1],))


def on_device(histories, bin_index, delays, map_adjoint):
    groups = lax.axis_size("grp")
    position = lax.axis_index("grp")
    bins = bin_index.shape[0]
    sensors = delays.shape[0] * lax.axis_size(SENS_AXES)
    steer_scale = 1.0 / math.sqrt(sensors)
    samples = histories.shape[1]
    scan_share = delays.shape[1] // groups

    transform = transform_rows(position * samples, samples, bin_index, NT)
    spectra = jnp.dot(histories, transform, preferred_element_type=jnp.float32)
    spectra = jnp.sum(gather_stack(spectra, "grp"), axis=0)
    real_t = spectra[:, :bins].T
    imag_t = spectra[:, bins:].T

    own_delays = lax.dynamic_slice_in_dim(delays, position * scan_share, scan_share, 1)
    own_weight = 2.0 * lax.dynamic_slice_in_dim(map_adjoint, position * scan_share, scan_share, 0)
    phase_index = (bin_index[:, None, None] * own_delays[None, :, :]) & (NT - 1)
    cosine, sine_part = lax.optimization_barrier(circle_point(phase_index, NT))

    steer_real = jnp.sum(real_t[:, :, None] * cosine - imag_t[:, :, None] * sine_part, axis=1)
    steer_imag = jnp.sum(real_t[:, :, None] * sine_part + imag_t[:, :, None] * cosine, axis=1)
    steered = jnp.stack([steer_real, steer_imag]) * steer_scale
    offset = 0
    for axis in SENS_AXES:
        offset = offset * lax.axis_size(axis) + lax.axis_index(axis)
    count = lax.axis_size(SENS_AXES)
    parts = steered.reshape(count, steered.size // count)
    width = parts.shape[1]
    chunk = jnp.sum(lax.all_to_all(parts, SENS_AXES, 0, 0, tiled=True), axis=0)
    start = (offset * width) % scan_share
    chunk = lax.dynamic_slice_in_dim(own_weight, start, width, 0) * chunk
    bar = lax.all_gather(chunk, SENS_AXES, tiled=True).reshape(steered.shape)
    bar_real = bar[0]
    bar_imag = bar[1]

    back_real = jnp.sum(bar_real[:, None, :] * cosine + bar_imag[:, None, :] * sine_part, axis=2)
    back_imag = jnp.sum(bar_imag[:, None, :] * cosine - bar_real[:, None, :] * sine_part, axis=2)
    back = jnp.concatenate([back_real.T, back_imag.T], 1) * steer_scale
    back = jnp.sum(gather_stack(back, "grp"), axis=0)
    adjoint = back.astype(jnp.bfloat16)
    local_part = lax.dot_general(
        adjoint, transform, (((1,), (1,)), ((), ())), preferred_element_type=jnp.float32
    )
    return local_part.astype(jnp.bfloat16)


SENS_AXES = ("sx", "sz", "sy")


def solution(mesh):
    sens_size = mesh.shape["sens"]
    side = round(sens_size ** (1.0 / 3.0))
    assert side ** 3 == sens_size
    fine = jax.sharding.Mesh(
        mesh.devices.reshape(side, side, side, mesh.shape["grp"]), SENS_AXES + ("grp",)
    )
    placed = (P(SENS_AXES, "grp"), P(), P(SENS_AXES, None), P())
    return jax.shard_map(
        on_device, mesh=fine, in_specs=placed, out_specs=P(SENS_AXES, "grp"), check_vma=False
    )
```

```python
import math

import jax
import jax.numpy as jnp
from jax import lax
from jax.sharding import PartitionSpec as P

NT = 4096

two_pi = 2.0 * math.pi


def transform_rows(first, count, bin_index, length):
    sample_times = first + lax.iota(jnp.int32, count)
    phase_index = sample_times[:, None] * bin_index[None, :] % length
    phase_angle = phase_index.astype(jnp.float32) * (two_pi / length)
    factor = 1.0 / math.sqrt(length)
    cosine = jnp.cos(phase_angle) * factor
    sine_part = -jnp.sin(phase_angle) * factor
    return jnp.concatenate([cosine, sine_part], 1).astype(jnp.bfloat16)


def circle_point(phase_index, length):
    eighth_bits = (length // 8).bit_length() - 1
    quarter = length // 4
    quadrant = phase_index >> (eighth_bits + 1)
    rest = phase_index & (quarter - 1)
    flip = (rest >> eighth_bits) & (rest != (length // 8)).astype(jnp.int32)
    folded = jnp.where(flip == 1, quarter - rest, rest)
    x = folded.astype(jnp.float32) * (two_pi / length)
    x2 = x * x
    sin_x = x * (1.0 + x2 * (-1.0 / 6.0 + x2 * (1.0 / 120.0 + x2 * (-1.0 / 5040.0))))
    cos_x = 1.0 + x2 * (-0.5 + x2 * (1.0 / 24.0 + x2 * (-1.0 / 720.0 + x2 * (1.0 / 40320.0))))
    swap = ((quadrant & 1) ^ flip) == 1
    sine = jnp.where(swap, cos_x, sin_x)
    cosine = jnp.where(swap, sin_x, cos_x)
    sine = jnp.where(quadrant >= 2, -sine, sine)
    cosine = jnp.where(((quadrant ^ (quadrant >> 1)) & 1) == 1, -cosine, cosine)
    return cosine, sine


def shifted(x, axis, shift):
    count = lax.axis_size(axis)
    return lax.ppermute(x, axis, [(j, (j + shift) % count) for j in range(count)])


def gather_stack(x, axis):
    count = lax.axis_size(axis)
    me = lax.axis_index(axis)
    stack = jnp.stack([x] + [shifted(x, axis, shift) for shift in range(1, count)])
    return stack[(me - jnp.arange(count)) % count]


def scatter_sum(x, axis):
    count = lax.axis_size(axis)
    lead = x.shape[:-1]
    parts = x.reshape(lead + (count, x.shape[-1] // count))
    parts = jnp.moveaxis(parts, -2, 0).reshape(count, -1)
    total = jnp.sum(lax.all_to_all(parts, axis, 0, 0, tiled=True), axis=0)
    return total.reshape(lead + (x.shape[-1] // count,))


def gather_last(x, axis):
    count = lax.axis_size(axis)
    copies = jnp.broadcast_to(x.reshape(1, -1), (count, x.size))
    joined = lax.all_to_all(copies, axis, 0, 0, tiled=True).reshape((count,) + x.shape)
    joined = jnp.moveaxis(joined, 0, -2)
    return joined.reshape(x.shape[:-1] + (count * x.shape[-1],))


def on_device(histories, bin_index, delays, map_adjoint):
    groups = lax.axis_size("grp")
    position = lax.axis_index("grp")
    bins = bin_index.shape[0]
    sensors = delays.shape[0] * lax.axis_size(SENS_AXES)
    steer_scale = 1.0 / math.sqrt(sensors)
    samples = histories.shape[1]
    scan_share = delays.shape[1] // groups

    transform = transform_rows(position * samples, samples, bin_index, NT)
    spectra = jnp.dot(histories, transform, preferred_element_type=jnp.float32)
    spectra = jnp.sum(gather_stack(spectra, "grp"), axis=0)
    real_t = spectra[:, :bins].T
    imag_t = spectra[:, bins:].T

    own_delays = lax.dynamic_slice_in_dim(delays, position * scan_share, scan_share, 1)
    own_weight = 2.0 * lax.dynamic_slice_in_dim(map_adjoint, position * scan_share, scan_share, 0)
    phase_index = (bin_index[:, None, None] * own_delays[None, :, :]) & (NT - 1)
    cosine, sine_part = lax.optimization_barrier(circle_point(phase_index, NT))

    steer_real = jnp.sum(real_t[:, :, None] * cosine - imag_t[:, :, None] * sine_part, axis=1)
    steer_imag = jnp.sum(real_t[:, :, None] * sine_part + imag_t[:, :, None] * cosine, axis=1)
    steered = jnp.stack([steer_real, steer_imag]) * steer_scale
    offset = 0
    for axis in SENS_AXES:
        offset = offset * lax.axis_size(axis) + lax.axis_index(axis)
    count = lax.axis_size(SENS_AXES)
    parts = steered.reshape(count, steered.size // count)
    width = parts.shape[1]
    chunk = jnp.sum(lax.all_to_all(parts, SENS_AXES, 0, 0, tiled=True), axis=0)
    start = (offset * width) % scan_share
    chunk = lax.dynamic_slice_in_dim(own_weight, start, width, 0) * chunk
    copies = jnp.broadcast_to(chunk[None], (count, width))
    bar = lax.all_to_all(copies, SENS_AXES, 0, 0, tiled=True).reshape(steered.shape)
    bar_real = bar[0]
    bar_imag = bar[1]

    back_real = jnp.sum(bar_real[:, None, :] * cosine + bar_imag[:, None, :] * sine_part, axis=2)
    back_imag = jnp.sum(bar_imag[:, None, :] * cosine - bar_real[:, None, :] * sine_part, axis=2)
    back = jnp.concatenate([back_real.T, back_imag.T], 1) * steer_scale
    back = jnp.sum(gather_stack(back, "grp"), axis=0)
    adjoint = back.astype(jnp.bfloat16)
    local_part = lax.dot_general(
        adjoint, transform, (((1,), (1,)), ((), ())), preferred_element_type=jnp.float32
    )
    return local_part.astype(jnp.bfloat16)


SENS_AXES = ("sx", "sz", "sy")


def solution(mesh):
    sens_size = mesh.shape["sens"]
    side = round(sens_size ** (1.0 / 3.0))
    assert side ** 3 == sens_size
    fine = jax.sharding.Mesh(
        mesh.devices.reshape(side, side, side, mesh.shape["grp"]), SENS_AXES + ("grp",)
    )
    placed = (P(SENS_AXES, "grp"), P(), P(SENS_AXES, None), P())
    return jax.shard_map(
        on_device, mesh=fine, in_specs=placed, out_specs=P(SENS_AXES, "grp"), check_vma=False
    )
```

```python
import math

import jax
import jax.numpy as jnp
from jax import lax
from jax.sharding import PartitionSpec as P

NT = 4096

two_pi = 2.0 * math.pi


def transform_rows(first, count, bin_index, length):
    sample_times = first + lax.iota(jnp.int32, count)
    phase_index = sample_times[:, None] * bin_index[None, :] % length
    phase_angle = phase_index.astype(jnp.float32) * (two_pi / length)
    factor = 1.0 / math.sqrt(length)
    cosine = jnp.cos(phase_angle) * factor
    sine_part = -jnp.sin(phase_angle) * factor
    return jnp.concatenate([cosine, sine_part], 1).astype(jnp.bfloat16)


def circle_point(phase_index, length):
    eighth_bits = (length // 8).bit_length() - 1
    quarter = length // 4
    quadrant = phase_index >> (eighth_bits + 1)
    rest = phase_index & (quarter - 1)
    flip = (rest >> eighth_bits) & (rest != (length // 8)).astype(jnp.int32)
    folded = jnp.where(flip == 1, quarter - rest, rest)
    x = folded.astype(jnp.float32) * (two_pi / length)
    x2 = x * x
    sin_x = x * (1.0 + x2 * (-1.0 / 6.0 + x2 * (1.0 / 120.0 + x2 * (-1.0 / 5040.0))))
    cos_x = 1.0 + x2 * (-0.5 + x2 * (1.0 / 24.0 + x2 * (-1.0 / 720.0 + x2 * (1.0 / 40320.0))))
    swap = ((quadrant & 1) ^ flip) == 1
    sine = jnp.where(swap, cos_x, sin_x)
    cosine = jnp.where(swap, sin_x, cos_x)
    sine = jnp.where(quadrant >= 2, -sine, sine)
    cosine = jnp.where(((quadrant ^ (quadrant >> 1)) & 1) == 1, -cosine, cosine)
    return cosine, sine


def shifted(x, axis, shift):
    count = lax.axis_size(axis)
    return lax.ppermute(x, axis, [(j, (j + shift) % count) for j in range(count)])


def gather_stack(x, axis):
    count = lax.axis_size(axis)
    me = lax.axis_index(axis)
    stack = jnp.stack([x] + [shifted(x, axis, shift) for shift in range(1, count)])
    return stack[(me - jnp.arange(count)) % count]


def scatter_sum(x, axis):
    count = lax.axis_size(axis)
    lead = x.shape[:-1]
    parts = x.reshape(lead + (count, x.shape[-1] // count))
    parts = jnp.moveaxis(parts, -2, 0).reshape(count, -1)
    total = jnp.sum(lax.all_to_all(parts, axis, 0, 0, tiled=True), axis=0)
    return total.reshape(lead + (x.shape[-1] // count,))


def gather_last(x, axis):
    count = lax.axis_size(axis)
    copies = jnp.broadcast_to(x.reshape(1, -1), (count, x.size))
    joined = lax.all_to_all(copies, axis, 0, 0, tiled=True).reshape((count,) + x.shape)
    joined = jnp.moveaxis(joined, 0, -2)
    return joined.reshape(x.shape[:-1] + (count * x.shape[-1],))


def on_device(histories, bin_index, delays, map_adjoint):
    groups = lax.axis_size("grp")
    position = lax.axis_index("grp")
    bins = bin_index.shape[0]
    sensors = delays.shape[0] * lax.axis_size(SENS_AXES)
    steer_scale = 1.0 / math.sqrt(sensors)
    samples = histories.shape[1]
    scan_share = delays.shape[1] // groups

    transform = transform_rows(position * samples, samples, bin_index, NT)
    spectra = jnp.dot(histories, transform, preferred_element_type=jnp.float32)
    spectra = jnp.sum(gather_stack(spectra, "grp"), axis=0)
    real_t = spectra[:, :bins].T
    imag_t = spectra[:, bins:].T

    own_delays = lax.dynamic_slice_in_dim(delays, position * scan_share, scan_share, 1)
    phase_index = (bin_index[:, None, None] * own_delays[None, :, :]) & (NT - 1)
    cosine, sine_part = lax.optimization_barrier(circle_point(phase_index, NT))

    steer_real = jnp.sum(real_t[:, :, None] * cosine - imag_t[:, :, None] * sine_part, axis=1)
    steer_imag = jnp.sum(real_t[:, :, None] * sine_part + imag_t[:, :, None] * cosine, axis=1)
    steered = jnp.stack([steer_real, steer_imag])
    offset = 0
    for axis in SENS_AXES:
        offset = offset * lax.axis_size(axis) + lax.axis_index(axis)
    count = lax.axis_size(SENS_AXES)
    parts = steered.reshape(count, steered.size // count)
    width = parts.shape[1]
    moved, held_weight = lax.optimization_barrier(
        (lax.all_to_all(parts, SENS_AXES, 0, 0, tiled=True), map_adjoint)
    )
    start = position * scan_share + (offset * width) % scan_share
    chunk_weight = (2.0 * steer_scale) * lax.dynamic_slice_in_dim(held_weight, start, width, 0)
    chunk = chunk_weight * jnp.sum(moved, axis=0)
    copies = jnp.broadcast_to(chunk[None], (count, width))
    bar = lax.all_to_all(copies, SENS_AXES, 0, 0, tiled=True).reshape(steered.shape)
    bar_real = bar[0]
    bar_imag = bar[1]

    back_real = jnp.sum(bar_real[:, None, :] * cosine + bar_imag[:, None, :] * sine_part, axis=2)
    back_imag = jnp.sum(bar_imag[:, None, :] * cosine - bar_real[:, None, :] * sine_part, axis=2)
    back = jnp.concatenate([back_real.T, back_imag.T], 1) * steer_scale
    back = jnp.sum(gather_stack(back, "grp"), axis=0)
    adjoint = back.astype(jnp.bfloat16)
    local_part = lax.dot_general(
        adjoint, transform, (((1,), (1,)), ((), ())), preferred_element_type=jnp.float32
    )
    return local_part.astype(jnp.bfloat16)


SENS_AXES = ("sx", "sz", "sy")


def solution(mesh):
    sens_size = mesh.shape["sens"]
    side = round(sens_size ** (1.0 / 3.0))
    assert side ** 3 == sens_size
    fine = jax.sharding.Mesh(
        mesh.devices.reshape(side, side, side, mesh.shape["grp"]), SENS_AXES + ("grp",)
    )
    placed = (P(SENS_AXES, "grp"), P(), P(SENS_AXES, None), P())
    return jax.shard_map(
        on_device, mesh=fine, in_specs=placed, out_specs=P(SENS_AXES, "grp"), check_vma=False
    )
```

```python
import math

import jax
import jax.numpy as jnp
from jax import lax
from jax.sharding import PartitionSpec as P

NT = 4096

two_pi = 2.0 * math.pi


def transform_rows(first, count, bin_index, length):
    sample_times = first + lax.iota(jnp.int32, count)
    phase_index = sample_times[:, None] * bin_index[None, :] % length
    phase_angle = phase_index.astype(jnp.float32) * (two_pi / length)
    factor = 1.0 / math.sqrt(length)
    cosine = jnp.cos(phase_angle) * factor
    sine_part = -jnp.sin(phase_angle) * factor
    return jnp.concatenate([cosine, sine_part], 1).astype(jnp.bfloat16)


def circle_point(phase_index, length):
    eighth_bits = (length // 8).bit_length() - 1
    quarter = length // 4
    quadrant = phase_index >> (eighth_bits + 1)
    rest = phase_index & (quarter - 1)
    flip = (rest >> eighth_bits) & (rest != (length // 8)).astype(jnp.int32)
    folded = jnp.where(flip == 1, quarter - rest, rest)
    x = folded.astype(jnp.float32) * (two_pi / length)
    x2 = x * x
    sin_x = x * (1.0 + x2 * (-1.0 / 6.0 + x2 * (1.0 / 120.0 + x2 * (-1.0 / 5040.0))))
    cos_x = 1.0 + x2 * (-0.5 + x2 * (1.0 / 24.0 + x2 * (-1.0 / 720.0 + x2 * (1.0 / 40320.0))))
    swap = ((quadrant & 1) ^ flip) == 1
    sine = jnp.where(swap, cos_x, sin_x)
    cosine = jnp.where(swap, sin_x, cos_x)
    sine = jnp.where(quadrant >= 2, -sine, sine)
    cosine = jnp.where(((quadrant ^ (quadrant >> 1)) & 1) == 1, -cosine, cosine)
    return cosine, sine


def shifted(x, axis, shift):
    count = lax.axis_size(axis)
    return lax.ppermute(x, axis, [(j, (j + shift) % count) for j in range(count)])


def ring_sum(x, axis):
    total = x
    for shift in range(1, lax.axis_size(axis)):
        total = total + shifted(x, axis, shift)
    return total


def gather_stack(x, axis):
    count = lax.axis_size(axis)
    me = lax.axis_index(axis)
    stack = jnp.stack([x] + [shifted(x, axis, shift) for shift in range(1, count)])
    return stack[(me - jnp.arange(count)) % count]


def scatter_sum(x, axis):
    count = lax.axis_size(axis)
    lead = x.shape[:-1]
    parts = x.reshape(lead + (count, x.shape[-1] // count))
    parts = jnp.moveaxis(parts, -2, 0).reshape(count, -1)
    total = jnp.sum(lax.all_to_all(parts, axis, 0, 0, tiled=True), axis=0)
    return total.reshape(lead + (x.shape[-1] // count,))


def gather_last(x, axis):
    count = lax.axis_size(axis)
    copies = jnp.broadcast_to(x.reshape(1, -1), (count, x.size))
    joined = lax.all_to_all(copies, axis, 0, 0, tiled=True).reshape((count,) + x.shape)
    joined = jnp.moveaxis(joined, 0, -2)
    return joined.reshape(x.shape[:-1] + (count * x.shape[-1],))


def on_device(histories, bin_index, delays, map_adjoint):
    groups = lax.axis_size("grp")
    position = lax.axis_index("grp")
    bins = bin_index.shape[0]
    sensors = delays.shape[0] * lax.axis_size(SENS_AXES)
    steer_scale = 1.0 / math.sqrt(sensors)
    samples = histories.shape[1]
    scan_share = delays.shape[1] // groups

    transform = transform_rows(position * samples, samples, bin_index, NT)
    spectra = jnp.dot(histories, transform, preferred_element_type=jnp.float32)
    spectra = ring_sum(spectra, "grp")
    real_t = spectra[:, :bins].T
    imag_t = spectra[:, bins:].T

    own_delays = lax.dynamic_slice_in_dim(delays, position * scan_share, scan_share, 1)
    phase_index = (bin_index[:, None, None] * own_delays[None, :, :]) & (NT - 1)
    cosine, sine_part = lax.optimization_barrier(circle_point(phase_index, NT))

    steer_real = jnp.sum(real_t[:, :, None] * cosine - imag_t[:, :, None] * sine_part, axis=1)
    steer_imag = jnp.sum(real_t[:, :, None] * sine_part + imag_t[:, :, None] * cosine, axis=1)
    steered = jnp.stack([steer_real, steer_imag])
    offset = 0
    for axis in SENS_AXES:
        offset = offset * lax.axis_size(axis) + lax.axis_index(axis)
    count = lax.axis_size(SENS_AXES)
    parts = steered.reshape(count, steered.size // count)
    width = parts.shape[1]
    start = position * scan_share + (offset * width) % scan_share
    chunk_weight = (2.0 * steer_scale) * lax.dynamic_slice_in_dim(map_adjoint, start, width, 0)
    parts, chunk_weight = lax.optimization_barrier((parts, chunk_weight))
    moved = lax.all_to_all(parts, SENS_AXES, 0, 0, tiled=True)
    chunk = chunk_weight * jnp.sum(moved, axis=0)
    copies = jnp.broadcast_to(chunk[None], (count, width))
    bar = lax.all_to_all(copies, SENS_AXES, 0, 0, tiled=True).reshape(steered.shape)
    bar_real = bar[0]
    bar_imag = bar[1]

    back_real = jnp.sum(bar_real[:, None, :] * cosine + bar_imag[:, None, :] * sine_part, axis=2)
    back_imag = jnp.sum(bar_imag[:, None, :] * cosine - bar_real[:, None, :] * sine_part, axis=2)
    back = jnp.concatenate([back_real.T, back_imag.T], 1) * steer_scale
    back = ring_sum(back, "grp")
    adjoint = back.astype(jnp.bfloat16)
    local_part = lax.dot_general(
        adjoint, transform, (((1,), (1,)), ((), ())), preferred_element_type=jnp.float32
    )
    return local_part.astype(jnp.bfloat16)


SENS_AXES = ("sx", "sz", "sy")


def solution(mesh):
    sens_size = mesh.shape["sens"]
    side = round(sens_size ** (1.0 / 3.0))
    assert side ** 3 == sens_size
    fine = jax.sharding.Mesh(
        mesh.devices.reshape(side, side, side, mesh.shape["grp"]), SENS_AXES + ("grp",)
    )
    placed = (P(SENS_AXES, "grp"), P(), P(SENS_AXES, None), P())
    return jax.shard_map(
        on_device, mesh=fine, in_specs=placed, out_specs=P(SENS_AXES, "grp"), check_vma=False
    )
```

```python
import math

import jax
import jax.numpy as jnp
from jax import lax
from jax.sharding import PartitionSpec as P
from jax.experimental import pallas as pl
from jax.experimental.pallas import tpu as pltpu
import functools

NT = 4096

two_pi = 2.0 * math.pi


def transform_rows(first, count, bin_index, length):
    sample_times = first + lax.iota(jnp.int32, count)
    phase_index = sample_times[:, None] * bin_index[None, :] % length
    phase_angle = phase_index.astype(jnp.float32) * (two_pi / length)
    factor = 1.0 / math.sqrt(length)
    cosine = jnp.cos(phase_angle) * factor
    sine_part = -jnp.sin(phase_angle) * factor
    return jnp.concatenate([cosine, sine_part], 1).astype(jnp.bfloat16)


def circle_point(phase_index, length):
    eighth_bits = (length // 8).bit_length() - 1
    quarter = length // 4
    quadrant = phase_index >> (eighth_bits + 1)
    rest = phase_index & (quarter - 1)
    flip = (rest >> eighth_bits) & (rest != (length // 8)).astype(jnp.int32)
    folded = jnp.where(flip == 1, quarter - rest, rest)
    x = folded.astype(jnp.float32) * (two_pi / length)
    x2 = x * x
    sin_x = x * (1.0 + x2 * (-1.0 / 6.0 + x2 * (1.0 / 120.0 + x2 * (-1.0 / 5040.0))))
    cos_x = 1.0 + x2 * (-0.5 + x2 * (1.0 / 24.0 + x2 * (-1.0 / 720.0 + x2 * (1.0 / 40320.0))))
    swap = ((quadrant & 1) ^ flip) == 1
    sine = jnp.where(swap, cos_x, sin_x)
    cosine = jnp.where(swap, sin_x, cos_x)
    sine = jnp.where(quadrant >= 2, -sine, sine)
    cosine = jnp.where(((quadrant ^ (quadrant >> 1)) & 1) == 1, -cosine, cosine)
    return cosine, sine


LANE_TILE = 128

def forward_kernel(length, bins_ref, delays_ref, xr_ref, xi_ref, cos_ref, sin_ref, steer_ref):
    group = cos_ref.shape[0]
    width = delays_ref.shape[1]
    first = pl.program_id(0) * group
    for i in range(group):
        b = bins_ref[first + i]
        xr = xr_ref[i]
        xi = xi_ref[i]
        for j in range(width // LANE_TILE):
            cols = pl.ds(j * LANE_TILE, LANE_TILE)
            k = (delays_ref[:, cols] * b) & (length - 1)
            c, s = circle_point(k, length)
            cos_ref[i, :, cols] = c
            sin_ref[i, :, cols] = s
            steer_ref[i, 0:1, cols] = jnp.sum(xr * c - xi * s, axis=0, keepdims=True)
            steer_ref[i, 1:2, cols] = jnp.sum(xr * s + xi * c, axis=0, keepdims=True)


BIN_GROUP = 4


def trig_forward(bin_index, delays, real_t, imag_t, length):
    bins = bin_index.shape[0]
    rows, width = delays.shape
    group = math.gcd(bins, BIN_GROUP)
    elems = bins * rows * width
    return pl.pallas_call(
        functools.partial(forward_kernel, length),
        grid=(bins // group,),
        out_shape=(
            jax.ShapeDtypeStruct((bins, rows, width), jnp.float32),
            jax.ShapeDtypeStruct((bins, rows, width), jnp.float32),
            jax.ShapeDtypeStruct((bins, 2, width), jnp.float32),
        ),
        in_specs=[
            pl.BlockSpec(memory_space=pltpu.SMEM),
            pl.BlockSpec((rows, width), lambda g: (0, 0)),
            pl.BlockSpec((group, rows, 1), lambda g: (g, 0, 0)),
            pl.BlockSpec((group, rows, 1), lambda g: (g, 0, 0)),
        ],
        out_specs=(
            pl.BlockSpec((group, rows, width), lambda g: (g, 0, 0)),
            pl.BlockSpec((group, rows, width), lambda g: (g, 0, 0)),
            pl.BlockSpec((group, 2, width), lambda g: (g, 0, 0)),
        ),
        cost_estimate=pl.CostEstimate(
            flops=60 * elems, transcendentals=0, bytes_accessed=8 * elems + 4 * rows * width
        ),
    )(bin_index, delays, real_t[:, :, None], imag_t[:, :, None])


def shifted(x, axis, shift):
    count = lax.axis_size(axis)
    return lax.ppermute(x, axis, [(j, (j + shift) % count) for j in range(count)])


def ring_sum(x, axis):
    total = x
    for shift in range(1, lax.axis_size(axis)):
        total = total + shifted(x, axis, shift)
    return total


def gather_stack(x, axis):
    count = lax.axis_size(axis)
    me = lax.axis_index(axis)
    stack = jnp.stack([x] + [shifted(x, axis, shift) for shift in range(1, count)])
    return stack[(me - jnp.arange(count)) % count]


def scatter_sum(x, axis):
    count = lax.axis_size(axis)
    lead = x.shape[:-1]
    parts = x.reshape(lead + (count, x.shape[-1] // count))
    parts = jnp.moveaxis(parts, -2, 0).reshape(count, -1)
    total = jnp.sum(lax.all_to_all(parts, axis, 0, 0, tiled=True), axis=0)
    return total.reshape(lead + (x.shape[-1] // count,))


def gather_last(x, axis):
    count = lax.axis_size(axis)
    copies = jnp.broadcast_to(x.reshape(1, -1), (count, x.size))
    joined = lax.all_to_all(copies, axis, 0, 0, tiled=True).reshape((count,) + x.shape)
    joined = jnp.moveaxis(joined, 0, -2)
    return joined.reshape(x.shape[:-1] + (count * x.shape[-1],))


def on_device(histories, bin_index, delays, map_adjoint):
    groups = lax.axis_size("grp")
    position = lax.axis_index("grp")
    bins = bin_index.shape[0]
    sensors = delays.shape[0] * lax.axis_size(SENS_AXES)
    steer_scale = 1.0 / math.sqrt(sensors)
    samples = histories.shape[1]
    scan_share = delays.shape[1] // groups

    transform = transform_rows(position * samples, samples, bin_index, NT)
    spectra = jnp.dot(histories, transform, preferred_element_type=jnp.float32)
    spectra = ring_sum(spectra, "grp")
    real_t = spectra[:, :bins].T
    imag_t = spectra[:, bins:].T

    own_delays = lax.dynamic_slice_in_dim(delays, position * scan_share, scan_share, 1)
    cosine, sine_part, steered = trig_forward(bin_index, own_delays, real_t, imag_t, NT)
    offset = 0
    for axis in SENS_AXES:
        offset = offset * lax.axis_size(axis) + lax.axis_index(axis)
    count = lax.axis_size(SENS_AXES)
    parts = steered.reshape(count, steered.size // count)
    width = parts.shape[1]
    start = position * scan_share + (offset * width) % scan_share
    chunk_weight = (2.0 * steer_scale) * lax.dynamic_slice_in_dim(map_adjoint, start, width, 0)
    parts, chunk_weight = lax.optimization_barrier((parts, chunk_weight))
    moved = lax.all_to_all(parts, SENS_AXES, 0, 0, tiled=True)
    chunk = chunk_weight * jnp.sum(moved, axis=0)
    copies = jnp.broadcast_to(chunk[None], (count, width))
    bar = lax.all_to_all(copies, SENS_AXES, 0, 0, tiled=True).reshape(steered.shape)
    bar_real = bar[:, 0]
    bar_imag = bar[:, 1]

    back_real = jnp.sum(bar_real[:, None, :] * cosine + bar_imag[:, None, :] * sine_part, axis=2)
    back_imag = jnp.sum(bar_imag[:, None, :] * cosine - bar_real[:, None, :] * sine_part, axis=2)
    back = jnp.concatenate([back_real.T, back_imag.T], 1) * steer_scale
    back = ring_sum(back, "grp")
    adjoint = back.astype(jnp.bfloat16)
    local_part = lax.dot_general(
        adjoint, transform, (((1,), (1,)), ((), ())), preferred_element_type=jnp.float32
    )
    return local_part.astype(jnp.bfloat16)


SENS_AXES = ("sx", "sz", "sy")


def solution(mesh):
    sens_size = mesh.shape["sens"]
    side = round(sens_size ** (1.0 / 3.0))
    assert side ** 3 == sens_size
    fine = jax.sharding.Mesh(
        mesh.devices.reshape(side, side, side, mesh.shape["grp"]), SENS_AXES + ("grp",)
    )
    placed = (P(SENS_AXES, "grp"), P(), P(SENS_AXES, None), P())
    return jax.shard_map(
        on_device, mesh=fine, in_specs=placed, out_specs=P(SENS_AXES, "grp"), check_vma=False
    )
```

```python
import math

import jax
import jax.numpy as jnp
from jax import lax
from jax.sharding import PartitionSpec as P

NT = 4096

two_pi = 2.0 * math.pi


def transform_rows(first, count, bin_index, length):
    sample_times = first + lax.iota(jnp.int32, count)
    phase_index = (sample_times[:, None] * bin_index[None, :]) & (length - 1)
    factor = 1.0 / math.sqrt(length)
    cosine, sine = circle_point(phase_index, length)
    cosine = cosine * factor
    sine_part = -sine * factor
    return jnp.concatenate([cosine, sine_part], 1).astype(jnp.bfloat16)


def circle_point(phase_index, length):
    quarter_bits = (length // 4).bit_length() - 1
    nearest = (phase_index + length // 8) >> quarter_bits
    rest = phase_index - (nearest << quarter_bits)
    x = rest.astype(jnp.float32) * (two_pi / length)
    x2 = x * x
    sin_x = x * (1.0 + x2 * (-1.0 / 6.0 + x2 * (1.0 / 120.0 + x2 * (-1.0 / 5040.0))))
    cos_x = 1.0 + x2 * (-0.5 + x2 * (1.0 / 24.0 + x2 * (-1.0 / 720.0 + x2 * (1.0 / 40320.0))))
    swap = (nearest & 1) == 1
    sine = jnp.where(swap, cos_x, sin_x)
    cosine = jnp.where(swap, sin_x, cos_x)
    sine = jnp.where((nearest & 2) != 0, -sine, sine)
    cosine = jnp.where(((nearest + 1) & 2) != 0, -cosine, cosine)
    return cosine, sine


def shifted(x, axis, shift):
    count = lax.axis_size(axis)
    return lax.ppermute(x, axis, [(j, (j + shift) % count) for j in range(count)])


def ring_sum(x, axis):
    total = x
    for shift in range(1, lax.axis_size(axis)):
        total = total + shifted(x, axis, shift)
    return total


def gather_stack(x, axis):
    count = lax.axis_size(axis)
    me = lax.axis_index(axis)
    stack = jnp.stack([x] + [shifted(x, axis, shift) for shift in range(1, count)])
    return stack[(me - jnp.arange(count)) % count]


def scatter_sum(x, axis):
    count = lax.axis_size(axis)
    lead = x.shape[:-1]
    parts = x.reshape(lead + (count, x.shape[-1] // count))
    parts = jnp.moveaxis(parts, -2, 0).reshape(count, -1)
    total = jnp.sum(lax.all_to_all(parts, axis, 0, 0, tiled=True), axis=0)
    return total.reshape(lead + (x.shape[-1] // count,))


def gather_last(x, axis):
    count = lax.axis_size(axis)
    copies = jnp.broadcast_to(x.reshape(1, -1), (count, x.size))
    joined = lax.all_to_all(copies, axis, 0, 0, tiled=True).reshape((count,) + x.shape)
    joined = jnp.moveaxis(joined, 0, -2)
    return joined.reshape(x.shape[:-1] + (count * x.shape[-1],))


def on_device(histories, bin_index, delays, map_adjoint):
    groups = lax.axis_size("grp")
    position = lax.axis_index("grp")
    bins = bin_index.shape[0]
    sensors = delays.shape[0] * lax.axis_size(SENS_AXES)
    steer_scale = 1.0 / math.sqrt(sensors)
    samples = histories.shape[1]
    scan_share = delays.shape[1] // groups

    transform = transform_rows(position * samples, samples, bin_index, NT)
    spectra = jnp.dot(histories, transform, preferred_element_type=jnp.float32)
    spectra = ring_sum(spectra, "grp")
    real_t = spectra[:, :bins].T
    imag_t = spectra[:, bins:].T

    own_delays = lax.dynamic_slice_in_dim(delays, position * scan_share, scan_share, 1)
    phase_index = (bin_index[:, None, None] * own_delays[None, :, :]) & (NT - 1)
    cosine, sine_part = lax.optimization_barrier(circle_point(phase_index, NT))

    steer_real = jnp.sum(real_t[:, :, None] * cosine - imag_t[:, :, None] * sine_part, axis=1)
    steer_imag = jnp.sum(real_t[:, :, None] * sine_part + imag_t[:, :, None] * cosine, axis=1)
    steered = jnp.stack([steer_real, steer_imag])
    offset = 0
    for axis in SENS_AXES:
        offset = offset * lax.axis_size(axis) + lax.axis_index(axis)
    count = lax.axis_size(SENS_AXES)
    parts = steered.reshape(count, steered.size // count)
    width = parts.shape[1]
    start = position * scan_share + (offset * width) % scan_share
    chunk_weight = (2.0 * steer_scale) * lax.dynamic_slice_in_dim(map_adjoint, start, width, 0)
    parts, chunk_weight = lax.optimization_barrier((parts, chunk_weight))
    moved = lax.all_to_all(parts, SENS_AXES, 0, 0, tiled=True)
    chunk = chunk_weight * jnp.sum(moved, axis=0)
    copies = jnp.broadcast_to(chunk[None], (count, width))
    bar = lax.all_to_all(copies, SENS_AXES, 0, 0, tiled=True).reshape(steered.shape)
    bar_real = bar[0]
    bar_imag = bar[1]

    back_real = jnp.sum(bar_real[:, None, :] * cosine + bar_imag[:, None, :] * sine_part, axis=2)
    back_imag = jnp.sum(bar_imag[:, None, :] * cosine - bar_real[:, None, :] * sine_part, axis=2)
    back = jnp.concatenate([back_real.T, back_imag.T], 1) * steer_scale
    back = ring_sum(back, "grp")
    adjoint = back.astype(jnp.bfloat16)
    local_part = lax.dot_general(
        adjoint, transform, (((1,), (1,)), ((), ())), preferred_element_type=jnp.float32
    )
    return local_part.astype(jnp.bfloat16)


SENS_AXES = ("sx", "sz", "sy")


def solution(mesh):
    sens_size = mesh.shape["sens"]
    side = round(sens_size ** (1.0 / 3.0))
    assert side ** 3 == sens_size
    fine = jax.sharding.Mesh(
        mesh.devices.reshape(side, side, side, mesh.shape["grp"]), SENS_AXES + ("grp",)
    )
    placed = (P(SENS_AXES, "grp"), P(), P(SENS_AXES, None), P())
    return jax.shard_map(
        on_device, mesh=fine, in_specs=placed, out_specs=P(SENS_AXES, "grp"), check_vma=False
    )
```

```python
import math

import jax
import jax.numpy as jnp
from jax import lax
from jax.sharding import PartitionSpec as P

NT = 4096

two_pi = 2.0 * math.pi


def transform_rows(first, count, bin_index, length):
    sample_times = first + lax.iota(jnp.int32, count)
    phase_index = (sample_times[:, None] * bin_index[None, :]) & (length - 1)
    factor = 1.0 / math.sqrt(length)
    cosine, sine = circle_point(phase_index, length)
    cosine = cosine * factor
    sine_part = -sine * factor
    return jnp.concatenate([cosine, sine_part], 1).astype(jnp.bfloat16)


def circle_point(phase_index, length):
    quarter_bits = (length // 4).bit_length() - 1
    nearest = (phase_index + length // 8) >> quarter_bits
    rest = phase_index - (nearest << quarter_bits)
    x = rest.astype(jnp.float32) * (two_pi / length)
    x2 = x * x
    sin_x = x * (1.0 + x2 * (-1.0 / 6.0 + x2 * (1.0 / 120.0 + x2 * (-1.0 / 5040.0))))
    cos_x = 1.0 + x2 * (-0.5 + x2 * (1.0 / 24.0 + x2 * (-1.0 / 720.0 + x2 * (1.0 / 40320.0))))
    swap = (nearest & 1) == 1
    sine = jnp.where(swap, cos_x, sin_x)
    cosine = jnp.where(swap, sin_x, cos_x)
    sine = jnp.where((nearest & 2) != 0, -sine, sine)
    cosine = jnp.where(((nearest + 1) & 2) != 0, -cosine, cosine)
    return cosine, sine


def shifted(x, axis, shift):
    count = lax.axis_size(axis)
    return lax.ppermute(x, axis, [(j, (j + shift) % count) for j in range(count)])


def ring_sum(x, axis):
    total = x
    for shift in range(1, lax.axis_size(axis)):
        total = total + shifted(x, axis, shift)
    return total


def gather_stack(x, axis):
    count = lax.axis_size(axis)
    me = lax.axis_index(axis)
    stack = jnp.stack([x] + [shifted(x, axis, shift) for shift in range(1, count)])
    return stack[(me - jnp.arange(count)) % count]


def scatter_sum(x, axis):
    count = lax.axis_size(axis)
    lead = x.shape[:-1]
    parts = x.reshape(lead + (count, x.shape[-1] // count))
    parts = jnp.moveaxis(parts, -2, 0).reshape(count, -1)
    total = jnp.sum(lax.all_to_all(parts, axis, 0, 0, tiled=True), axis=0)
    return total.reshape(lead + (x.shape[-1] // count,))


def gather_last(x, axis):
    count = lax.axis_size(axis)
    copies = jnp.broadcast_to(x.reshape(1, -1), (count, x.size))
    joined = lax.all_to_all(copies, axis, 0, 0, tiled=True).reshape((count,) + x.shape)
    joined = jnp.moveaxis(joined, 0, -2)
    return joined.reshape(x.shape[:-1] + (count * x.shape[-1],))


def on_device(histories, bin_index, delays, map_adjoint):
    groups = lax.axis_size("grp")
    position = lax.axis_index("grp")
    bins = bin_index.shape[0]
    sensors = delays.shape[0] * lax.axis_size(SENS_AXES)
    steer_scale = 1.0 / math.sqrt(sensors)
    samples = histories.shape[1]
    scan_share = delays.shape[1] // groups

    transform = transform_rows(position * samples, samples, bin_index, NT)
    spectra = jnp.dot(histories, transform, preferred_element_type=jnp.float32)
    spectra = ring_sum(spectra, "grp")
    real_t = spectra[:, :bins].T
    imag_t = spectra[:, bins:].T

    own_delays = lax.dynamic_slice_in_dim(delays, position * scan_share, scan_share, 1)
    phase_index = (bin_index[:, None, None] * own_delays[None, :, :]) & (NT - 1)
    cosine, sine_part = lax.optimization_barrier(circle_point(phase_index, NT))

    steer_real = jnp.sum(real_t[:, :, None] * cosine - imag_t[:, :, None] * sine_part, axis=1)
    steer_imag = jnp.sum(real_t[:, :, None] * sine_part + imag_t[:, :, None] * cosine, axis=1)
    steered = jnp.stack([steer_real, steer_imag])
    offset = 0
    for axis in SENS_AXES:
        offset = offset * lax.axis_size(axis) + lax.axis_index(axis)
    count = lax.axis_size(SENS_AXES)
    parts = steered.reshape(count, steered.size // count)
    width = parts.shape[1]
    own_weight = (2.0 * steer_scale) * lax.dynamic_slice_in_dim(
        map_adjoint, position * scan_share, scan_share, 0
    )
    parts, own_weight = lax.optimization_barrier((parts, own_weight))
    moved = lax.all_to_all(parts, SENS_AXES, 0, 0, tiled=True)
    chunk = jnp.sum(moved, axis=0)
    copies = jnp.broadcast_to(chunk[None], (count, width))
    gathered = lax.all_to_all(copies, SENS_AXES, 0, 0, tiled=True).reshape(steered.shape)
    bar = own_weight * gathered
    bar_real = bar[0]
    bar_imag = bar[1]

    back_real = jnp.sum(bar_real[:, None, :] * cosine + bar_imag[:, None, :] * sine_part, axis=2)
    back_imag = jnp.sum(bar_imag[:, None, :] * cosine - bar_real[:, None, :] * sine_part, axis=2)
    back = jnp.concatenate([back_real.T, back_imag.T], 1) * steer_scale
    back = ring_sum(back, "grp")
    adjoint = back.astype(jnp.bfloat16)
    local_part = lax.dot_general(
        adjoint, transform, (((1,), (1,)), ((), ())), preferred_element_type=jnp.float32
    )
    return local_part.astype(jnp.bfloat16)


SENS_AXES = ("sx", "sz", "sy")


def solution(mesh):
    sens_size = mesh.shape["sens"]
    side = round(sens_size ** (1.0 / 3.0))
    assert side ** 3 == sens_size
    fine = jax.sharding.Mesh(
        mesh.devices.reshape(side, side, side, mesh.shape["grp"]), SENS_AXES + ("grp",)
    )
    placed = (P(SENS_AXES, "grp"), P(), P(SENS_AXES, None), P())
    return jax.shard_map(
        on_device, mesh=fine, in_specs=placed, out_specs=P(SENS_AXES, "grp"), check_vma=False
    )
```

```python
import math

import jax
import jax.numpy as jnp
from jax import lax
from jax.sharding import PartitionSpec as P

NT = 4096

two_pi = 2.0 * math.pi


def transform_rows(first, count, bin_index, length):
    sample_times = first + lax.iota(jnp.int32, count)
    phase_index = (sample_times[:, None] * bin_index[None, :]) & (length - 1)
    factor = 1.0 / math.sqrt(length)
    cosine, sine = circle_point(phase_index, length)
    cosine = cosine * factor
    sine_part = -sine * factor
    return jnp.concatenate([cosine, sine_part], 1).astype(jnp.bfloat16)


def circle_point(phase_index, length):
    quarter_bits = (length // 4).bit_length() - 1
    nearest = (phase_index + length // 8) >> quarter_bits
    rest = phase_index - (nearest << quarter_bits)
    x = rest.astype(jnp.float32) * (two_pi / length)
    x2 = x * x
    sin_x = x * (1.0 + x2 * (-1.0 / 6.0 + x2 * (1.0 / 120.0 + x2 * (-1.0 / 5040.0))))
    cos_x = 1.0 + x2 * (-0.5 + x2 * (1.0 / 24.0 + x2 * (-1.0 / 720.0 + x2 * (1.0 / 40320.0))))
    swap = (nearest & 1) == 1
    sine = jnp.where(swap, cos_x, sin_x)
    cosine = jnp.where(swap, sin_x, cos_x)
    sine = jnp.where((nearest & 2) != 0, -sine, sine)
    cosine = jnp.where(((nearest + 1) & 2) != 0, -cosine, cosine)
    return cosine, sine


def shifted(x, axis, shift):
    count = lax.axis_size(axis)
    return lax.ppermute(x, axis, [(j, (j + shift) % count) for j in range(count)])


def ring_sum(x, axis):
    total = x
    for shift in range(1, lax.axis_size(axis)):
        total = total + shifted(x, axis, shift)
    return total


def gather_stack(x, axis):
    count = lax.axis_size(axis)
    me = lax.axis_index(axis)
    stack = jnp.stack([x] + [shifted(x, axis, shift) for shift in range(1, count)])
    return stack[(me - jnp.arange(count)) % count]


def scatter_sum(x, axis):
    count = lax.axis_size(axis)
    lead = x.shape[:-1]
    parts = x.reshape(lead + (count, x.shape[-1] // count))
    parts = jnp.moveaxis(parts, -2, 0).reshape(count, -1)
    total = jnp.sum(lax.all_to_all(parts, axis, 0, 0, tiled=True), axis=0)
    return total.reshape(lead + (x.shape[-1] // count,))


def gather_last(x, axis):
    count = lax.axis_size(axis)
    copies = jnp.broadcast_to(x.reshape(1, -1), (count, x.size))
    joined = lax.all_to_all(copies, axis, 0, 0, tiled=True).reshape((count,) + x.shape)
    joined = jnp.moveaxis(joined, 0, -2)
    return joined.reshape(x.shape[:-1] + (count * x.shape[-1],))


def on_device(histories, bin_index, delays, map_adjoint):
    position = lax.axis_index("grp")
    bins = bin_index.shape[0]
    sensors = delays.shape[0] * lax.axis_size(SENS_AXES)
    steer_scale = 1.0 / math.sqrt(sensors)
    samples = histories.shape[1]

    transform = transform_rows(position * samples, samples, bin_index, NT)
    spectra = jnp.dot(histories, transform, preferred_element_type=jnp.float32)
    spectra = ring_sum(spectra, "grp")
    real_t = spectra[:, :bins].T
    imag_t = spectra[:, bins:].T

    own_delays = delays
    phase_index = (bin_index[:, None, None] * own_delays[None, :, :]) & (NT - 1)
    cosine, sine_part = lax.optimization_barrier(circle_point(phase_index, NT))

    steer_real = jnp.sum(real_t[:, :, None] * cosine - imag_t[:, :, None] * sine_part, axis=1)
    steer_imag = jnp.sum(real_t[:, :, None] * sine_part + imag_t[:, :, None] * cosine, axis=1)
    steered = jnp.stack([steer_real, steer_imag])
    offset = 0
    for axis in SENS_AXES:
        offset = offset * lax.axis_size(axis) + lax.axis_index(axis)
    count = lax.axis_size(SENS_AXES)
    parts = steered.reshape(count, steered.size // count)
    width = parts.shape[1]
    own_weight = (2.0 * steer_scale) * map_adjoint
    parts, own_weight = lax.optimization_barrier((parts, own_weight))
    moved = lax.all_to_all(parts, SENS_AXES, 0, 0, tiled=True)
    chunk = jnp.sum(moved, axis=0)
    copies = jnp.broadcast_to(chunk[None], (count, width))
    gathered = lax.all_to_all(copies, SENS_AXES, 0, 0, tiled=True).reshape(steered.shape)
    bar = own_weight * gathered
    bar_real = bar[0]
    bar_imag = bar[1]

    back_real = jnp.sum(bar_real[:, None, :] * cosine + bar_imag[:, None, :] * sine_part, axis=2)
    back_imag = jnp.sum(bar_imag[:, None, :] * cosine - bar_real[:, None, :] * sine_part, axis=2)
    back = jnp.concatenate([back_real.T, back_imag.T], 1) * steer_scale
    back = ring_sum(back, "grp")
    adjoint = back.astype(jnp.bfloat16)
    local_part = lax.dot_general(
        adjoint, transform, (((1,), (1,)), ((), ())), preferred_element_type=jnp.float32
    )
    return local_part.astype(jnp.bfloat16)


SENS_AXES = ("sx", "sz", "sy")


def solution(mesh):
    sens_size = mesh.shape["sens"]
    side = round(sens_size ** (1.0 / 3.0))
    assert side ** 3 == sens_size
    fine = jax.sharding.Mesh(
        mesh.devices.reshape(side, side, side, mesh.shape["grp"]), SENS_AXES + ("grp",)
    )
    placed = (P(SENS_AXES, "grp"), P(), P(SENS_AXES, "grp"), P("grp"))
    return jax.shard_map(
        on_device, mesh=fine, in_specs=placed, out_specs=P(SENS_AXES, "grp"), check_vma=False
    )
```

```python
import math

import jax
import jax.numpy as jnp
from jax import lax
from jax.sharding import PartitionSpec as P

NT = 4096

two_pi = 2.0 * math.pi


def transform_rows(first, count, bin_index, length):
    sample_times = first + lax.iota(jnp.int32, count)
    phase_index = (sample_times[:, None] * bin_index[None, :]) & (length - 1)
    factor = 1.0 / math.sqrt(length)
    cosine, sine = circle_point(phase_index, length)
    cosine = cosine * factor
    sine_part = -sine * factor
    return jnp.concatenate([cosine, sine_part], 1).astype(jnp.bfloat16)


def circle_point(phase_index, length):
    quarter_bits = (length // 4).bit_length() - 1
    nearest = (phase_index + length // 8) >> quarter_bits
    rest = phase_index - (nearest << quarter_bits)
    x = rest.astype(jnp.float32) * (two_pi / length)
    x2 = x * x
    sin_x = x * (1.0 + x2 * (-1.0 / 6.0 + x2 * (1.0 / 120.0 + x2 * (-1.0 / 5040.0))))
    cos_x = 1.0 + x2 * (-0.5 + x2 * (1.0 / 24.0 + x2 * (-1.0 / 720.0 + x2 * (1.0 / 40320.0))))
    swap = (nearest & 1) == 1
    sine = jnp.where(swap, cos_x, sin_x)
    cosine = jnp.where(swap, sin_x, cos_x)
    sine = jnp.where((nearest & 2) != 0, -sine, sine)
    cosine = jnp.where(((nearest + 1) & 2) != 0, -cosine, cosine)
    return cosine, sine


def shifted(x, axis, shift):
    count = lax.axis_size(axis)
    return lax.ppermute(x, axis, [(j, (j + shift) % count) for j in range(count)])


def ring_sum(x, axis):
    total = x
    for shift in range(1, lax.axis_size(axis)):
        total = total + shifted(x, axis, shift)
    return total


def gather_stack(x, axis):
    count = lax.axis_size(axis)
    me = lax.axis_index(axis)
    stack = jnp.stack([x] + [shifted(x, axis, shift) for shift in range(1, count)])
    return stack[(me - jnp.arange(count)) % count]


def scatter_sum(x, axis):
    count = lax.axis_size(axis)
    lead = x.shape[:-1]
    parts = x.reshape(lead + (count, x.shape[-1] // count))
    parts = jnp.moveaxis(parts, -2, 0).reshape(count, -1)
    total = jnp.sum(lax.all_to_all(parts, axis, 0, 0, tiled=True), axis=0)
    return total.reshape(lead + (x.shape[-1] // count,))


def gather_last(x, axis):
    count = lax.axis_size(axis)
    copies = jnp.broadcast_to(x.reshape(1, -1), (count, x.size))
    joined = lax.all_to_all(copies, axis, 0, 0, tiled=True).reshape((count,) + x.shape)
    joined = jnp.moveaxis(joined, 0, -2)
    return joined.reshape(x.shape[:-1] + (count * x.shape[-1],))


def on_device(histories, bin_index, delays, map_adjoint):
    groups = lax.axis_size("grp")
    position = lax.axis_index("grp")
    bins = bin_index.shape[0]
    sensors = delays.shape[0] * lax.axis_size(SENS_AXES)
    steer_scale = 1.0 / math.sqrt(sensors)
    samples = histories.shape[1]
    scan_share = delays.shape[1] // groups

    transform = transform_rows(position * samples, samples, bin_index, NT)
    spectra = jnp.dot(histories, transform, preferred_element_type=jnp.float32)
    spectra = ring_sum(spectra, "grp")
    real_t = spectra[:, :bins].T
    imag_t = spectra[:, bins:].T

    own_delays = lax.dynamic_slice_in_dim(delays, position * scan_share, scan_share, 1)
    phase_index = (bin_index[:, None, None] * own_delays[None, :, :]) & (NT - 1)
    cosine, sine_part = lax.optimization_barrier(circle_point(phase_index, NT))

    steer_real = jnp.sum(real_t[:, :, None] * cosine - imag_t[:, :, None] * sine_part, axis=1)
    steer_imag = jnp.sum(real_t[:, :, None] * sine_part + imag_t[:, :, None] * cosine, axis=1)
    steered = jnp.stack([steer_real, steer_imag])
    offset = 0
    for axis in SENS_AXES:
        offset = offset * lax.axis_size(axis) + lax.axis_index(axis)
    count = lax.axis_size(SENS_AXES)
    parts = steered.reshape(count, steered.size // count)
    width = parts.shape[1]
    own_weight = (2.0 * steer_scale) * lax.dynamic_slice_in_dim(
        map_adjoint, position * scan_share, scan_share, 0
    )
    parts, own_weight = lax.optimization_barrier((parts, own_weight))
    moved = lax.all_to_all(parts, EXCHANGE_ORDER, 0, 0, tiled=True)
    chunk = jnp.sum(moved, axis=0)
    copies = jnp.broadcast_to(chunk[None], (count, width))
    gathered = lax.all_to_all(copies, EXCHANGE_ORDER, 0, 0, tiled=True).reshape(steered.shape)
    bar = own_weight * gathered
    bar_real = bar[0]
    bar_imag = bar[1]

    back_real = jnp.sum(bar_real[:, None, :] * cosine + bar_imag[:, None, :] * sine_part, axis=2)
    back_imag = jnp.sum(bar_imag[:, None, :] * cosine - bar_real[:, None, :] * sine_part, axis=2)
    back = jnp.concatenate([back_real.T, back_imag.T], 1) * steer_scale
    back = ring_sum(back, "grp")
    adjoint = back.astype(jnp.bfloat16)
    local_part = lax.dot_general(
        adjoint, transform, (((1,), (1,)), ((), ())), preferred_element_type=jnp.float32
    )
    return local_part.astype(jnp.bfloat16)


SENS_AXES = ("sx", "sz", "sy")
EXCHANGE_ORDER = ("sy", "sz", "sx")


def solution(mesh):
    sens_size = mesh.shape["sens"]
    side = round(sens_size ** (1.0 / 3.0))
    assert side ** 3 == sens_size
    fine = jax.sharding.Mesh(
        mesh.devices.reshape(side, side, side, mesh.shape["grp"]), SENS_AXES + ("grp",)
    )
    placed = (P(SENS_AXES, "grp"), P(), P(SENS_AXES, None), P())
    return jax.shard_map(
        on_device, mesh=fine, in_specs=placed, out_specs=P(SENS_AXES, "grp"), check_vma=False
    )
```

```python
import math

import jax
import jax.numpy as jnp
from jax import lax
from jax.sharding import PartitionSpec as P

NT = 4096

two_pi = 2.0 * math.pi


def transform_rows(first, count, bin_index, length):
    sample_times = first + lax.iota(jnp.int32, count)
    phase_index = (sample_times[:, None] * bin_index[None, :]) & (length - 1)
    factor = 1.0 / math.sqrt(length)
    cosine, sine = circle_point(phase_index, length)
    cosine = cosine * factor
    sine_part = -sine * factor
    return jnp.concatenate([cosine, sine_part], 1).astype(jnp.bfloat16)


def circle_point(phase_index, length):
    quarter_bits = (length // 4).bit_length() - 1
    nearest = (phase_index + length // 8) >> quarter_bits
    rest = phase_index - (nearest << quarter_bits)
    x = rest.astype(jnp.float32) * (two_pi / length)
    x2 = x * x
    sin_x = x * (1.0 + x2 * (-1.0 / 6.0 + x2 * (1.0 / 120.0 + x2 * (-1.0 / 5040.0))))
    cos_x = 1.0 + x2 * (-0.5 + x2 * (1.0 / 24.0 + x2 * (-1.0 / 720.0 + x2 * (1.0 / 40320.0))))
    swap = (nearest & 1) == 1
    sine = jnp.where(swap, cos_x, sin_x)
    cosine = jnp.where(swap, sin_x, cos_x)
    sine = jnp.where((nearest & 2) != 0, -sine, sine)
    cosine = jnp.where(((nearest + 1) & 2) != 0, -cosine, cosine)
    return cosine, sine


def shifted(x, axis, shift):
    count = lax.axis_size(axis)
    return lax.ppermute(x, axis, [(j, (j + shift) % count) for j in range(count)])


def ring_sum(x, axis):
    total = x
    for shift in range(1, lax.axis_size(axis)):
        total = total + shifted(x, axis, shift)
    return total


def butterfly_sum(x, axis):
    count = lax.axis_size(axis)
    step = 1
    while step < count:
        x = x + lax.ppermute(x, axis, [(j, j ^ step) for j in range(count)])
        step *= 2
    return x


def gather_stack(x, axis):
    count = lax.axis_size(axis)
    me = lax.axis_index(axis)
    stack = jnp.stack([x] + [shifted(x, axis, shift) for shift in range(1, count)])
    return stack[(me - jnp.arange(count)) % count]


def scatter_sum(x, axis):
    count = lax.axis_size(axis)
    lead = x.shape[:-1]
    parts = x.reshape(lead + (count, x.shape[-1] // count))
    parts = jnp.moveaxis(parts, -2, 0).reshape(count, -1)
    total = jnp.sum(lax.all_to_all(parts, axis, 0, 0, tiled=True), axis=0)
    return total.reshape(lead + (x.shape[-1] // count,))


def gather_last(x, axis):
    count = lax.axis_size(axis)
    copies = jnp.broadcast_to(x.reshape(1, -1), (count, x.size))
    joined = lax.all_to_all(copies, axis, 0, 0, tiled=True).reshape((count,) + x.shape)
    joined = jnp.moveaxis(joined, 0, -2)
    return joined.reshape(x.shape[:-1] + (count * x.shape[-1],))


def on_device(histories, bin_index, delays, map_adjoint):
    groups = lax.axis_size("grp")
    position = lax.axis_index("grp")
    bins = bin_index.shape[0]
    sensors = delays.shape[0] * lax.axis_size(SENS_AXES)
    steer_scale = 1.0 / math.sqrt(sensors)
    samples = histories.shape[1]
    scan_share = delays.shape[1] // groups

    transform = transform_rows(position * samples, samples, bin_index, NT)
    spectra = jnp.dot(histories, transform, preferred_element_type=jnp.float32)
    spectra = ring_sum(spectra, "grp")
    real_t = spectra[:, :bins].T
    imag_t = spectra[:, bins:].T

    own_delays = lax.dynamic_slice_in_dim(delays, position * scan_share, scan_share, 1)
    phase_index = (bin_index[:, None, None] * own_delays[None, :, :]) & (NT - 1)
    cosine, sine_part = lax.optimization_barrier(circle_point(phase_index, NT))

    steer_real = jnp.sum(real_t[:, :, None] * cosine - imag_t[:, :, None] * sine_part, axis=1)
    steer_imag = jnp.sum(real_t[:, :, None] * sine_part + imag_t[:, :, None] * cosine, axis=1)
    steered = jnp.stack([steer_real, steer_imag])
    offset = 0
    for axis in SENS_AXES:
        offset = offset * lax.axis_size(axis) + lax.axis_index(axis)
    count = lax.axis_size(SENS_AXES)
    parts = steered.reshape(count, steered.size // count)
    width = parts.shape[1]
    own_weight = (2.0 * steer_scale) * lax.dynamic_slice_in_dim(
        map_adjoint, position * scan_share, scan_share, 0
    )
    parts, own_weight = lax.optimization_barrier((parts, own_weight))
    moved = lax.all_to_all(parts, SENS_AXES, 0, 0, tiled=True)
    chunk = jnp.sum(moved, axis=0)
    copies = jnp.broadcast_to(chunk[None], (count, width))
    gathered = lax.all_to_all(copies, SENS_AXES, 0, 0, tiled=True).reshape(steered.shape)
    bar = own_weight * gathered
    bar_real = bar[0]
    bar_imag = bar[1]

    back_real = jnp.sum(bar_real[:, None, :] * cosine + bar_imag[:, None, :] * sine_part, axis=2)
    back_imag = jnp.sum(bar_imag[:, None, :] * cosine - bar_real[:, None, :] * sine_part, axis=2)
    back = jnp.concatenate([back_real.T, back_imag.T], 1) * steer_scale
    back = butterfly_sum(back, "grp")
    adjoint = back.astype(jnp.bfloat16)
    local_part = lax.dot_general(
        adjoint, transform, (((1,), (1,)), ((), ())), preferred_element_type=jnp.float32
    )
    return local_part.astype(jnp.bfloat16)


SENS_AXES = ("sx", "sz", "sy")


def solution(mesh):
    sens_size = mesh.shape["sens"]
    side = round(sens_size ** (1.0 / 3.0))
    assert side ** 3 == sens_size
    fine = jax.sharding.Mesh(
        mesh.devices.reshape(side, side, side, mesh.shape["grp"]), SENS_AXES + ("grp",)
    )
    placed = (P(SENS_AXES, "grp"), P(), P(SENS_AXES, None), P())
    return jax.shard_map(
        on_device, mesh=fine, in_specs=placed, out_specs=P(SENS_AXES, "grp"), check_vma=False
    )
```

```python
import math

import jax
import jax.numpy as jnp
from jax import lax
from jax.sharding import PartitionSpec as P

NT = 4096

two_pi = 2.0 * math.pi


def transform_rows(first, count, bin_index, length):
    sample_times = first + lax.iota(jnp.int32, count)
    phase_index = sample_times[:, None] * bin_index[None, :]
    factor = 1.0 / math.sqrt(length)
    cosine, sine = circle_point(phase_index, length)
    cosine = cosine * factor
    sine_part = -sine * factor
    return jnp.concatenate([cosine, sine_part], 1).astype(jnp.bfloat16)


def circle_point(phase_index, length):
    quarter_bits = (length // 4).bit_length() - 1
    shifted_index = phase_index + length // 8
    nearest = shifted_index >> quarter_bits
    rest = (shifted_index & (length // 4 - 1)) - length // 8
    x = rest.astype(jnp.float32) * (two_pi / length)
    x2 = x * x
    sin_x = x * (1.0 + x2 * (-1.0 / 6.0 + x2 * (1.0 / 120.0 + x2 * (-1.0 / 5040.0))))
    cos_x = 1.0 + x2 * (-0.5 + x2 * (1.0 / 24.0 + x2 * (-1.0 / 720.0 + x2 * (1.0 / 40320.0))))
    swap = (nearest & 1) == 1
    sine = jnp.where(swap, cos_x, sin_x)
    cosine = jnp.where(swap, sin_x, cos_x)
    sine = jnp.where((nearest & 2) != 0, -sine, sine)
    cosine = jnp.where(((nearest + 1) & 2) != 0, -cosine, cosine)
    return cosine, sine


def shifted(x, axis, shift):
    count = lax.axis_size(axis)
    return lax.ppermute(x, axis, [(j, (j + shift) % count) for j in range(count)])


def ring_sum(x, axis):
    total = x
    for shift in range(1, lax.axis_size(axis)):
        total = total + shifted(x, axis, shift)
    return total


def gather_stack(x, axis):
    count = lax.axis_size(axis)
    me = lax.axis_index(axis)
    stack = jnp.stack([x] + [shifted(x, axis, shift) for shift in range(1, count)])
    return stack[(me - jnp.arange(count)) % count]


def scatter_sum(x, axis):
    count = lax.axis_size(axis)
    lead = x.shape[:-1]
    parts = x.reshape(lead + (count, x.shape[-1] // count))
    parts = jnp.moveaxis(parts, -2, 0).reshape(count, -1)
    total = jnp.sum(lax.all_to_all(parts, axis, 0, 0, tiled=True), axis=0)
    return total.reshape(lead + (x.shape[-1] // count,))


def gather_last(x, axis):
    count = lax.axis_size(axis)
    copies = jnp.broadcast_to(x.reshape(1, -1), (count, x.size))
    joined = lax.all_to_all(copies, axis, 0, 0, tiled=True).reshape((count,) + x.shape)
    joined = jnp.moveaxis(joined, 0, -2)
    return joined.reshape(x.shape[:-1] + (count * x.shape[-1],))


def on_device(histories, bin_index, delays, map_adjoint):
    groups = lax.axis_size("grp")
    position = lax.axis_index("grp")
    bins = bin_index.shape[0]
    sensors = delays.shape[0] * lax.axis_size(SENS_AXES)
    steer_scale = 1.0 / math.sqrt(sensors)
    samples = histories.shape[1]
    scan_share = delays.shape[1] // groups

    transform = transform_rows(position * samples, samples, bin_index, NT)
    spectra = jnp.dot(histories, transform, preferred_element_type=jnp.float32)
    spectra = ring_sum(spectra, "grp")
    real_t = spectra[:, :bins].T
    imag_t = spectra[:, bins:].T

    own_delays = lax.dynamic_slice_in_dim(delays, position * scan_share, scan_share, 1)
    phase_index = bin_index[:, None, None] * own_delays[None, :, :]
    cosine, sine_part = lax.optimization_barrier(circle_point(phase_index, NT))

    steer_real = jnp.sum(real_t[:, :, None] * cosine - imag_t[:, :, None] * sine_part, axis=1)
    steer_imag = jnp.sum(real_t[:, :, None] * sine_part + imag_t[:, :, None] * cosine, axis=1)
    steered = jnp.stack([steer_real, steer_imag])
    offset = 0
    for axis in SENS_AXES:
        offset = offset * lax.axis_size(axis) + lax.axis_index(axis)
    count = lax.axis_size(SENS_AXES)
    parts = steered.reshape(count, steered.size // count)
    width = parts.shape[1]
    own_weight = (2.0 * steer_scale) * lax.dynamic_slice_in_dim(
        map_adjoint, position * scan_share, scan_share, 0
    )
    parts, own_weight = lax.optimization_barrier((parts, own_weight))
    moved = lax.all_to_all(parts, SENS_AXES, 0, 0, tiled=True)
    chunk = jnp.sum(moved, axis=0)
    copies = jnp.broadcast_to(chunk[None], (count, width))
    gathered = lax.all_to_all(copies, SENS_AXES, 0, 0, tiled=True).reshape(steered.shape)
    bar = own_weight * gathered
    bar_real = bar[0]
    bar_imag = bar[1]

    back_real = jnp.sum(bar_real[:, None, :] * cosine + bar_imag[:, None, :] * sine_part, axis=2)
    back_imag = jnp.sum(bar_imag[:, None, :] * cosine - bar_real[:, None, :] * sine_part, axis=2)
    back = jnp.concatenate([back_real.T, back_imag.T], 1) * steer_scale
    back = ring_sum(back, "grp")
    adjoint = back.astype(jnp.bfloat16)
    local_part = lax.dot_general(
        adjoint, transform, (((1,), (1,)), ((), ())), preferred_element_type=jnp.float32
    )
    return local_part.astype(jnp.bfloat16)


SENS_AXES = ("sx", "sz", "sy")


def solution(mesh):
    sens_size = mesh.shape["sens"]
    side = round(sens_size ** (1.0 / 3.0))
    assert side ** 3 == sens_size
    fine = jax.sharding.Mesh(
        mesh.devices.reshape(side, side, side, mesh.shape["grp"]), SENS_AXES + ("grp",)
    )
    placed = (P(SENS_AXES, "grp"), P(), P(SENS_AXES, None), P())
    return jax.shard_map(
        on_device, mesh=fine, in_specs=placed, out_specs=P(SENS_AXES, "grp"), check_vma=False
    )
```

```python
import math

import jax
import jax.numpy as jnp
from jax import lax
from jax.sharding import PartitionSpec as P

NT = 4096

two_pi = 2.0 * math.pi


def transform_rows(first, count, bin_index, length):
    sample_times = first + lax.iota(jnp.int32, count)
    phase_index = sample_times[:, None] * bin_index[None, :]
    factor = 1.0 / math.sqrt(length)
    cosine, sine = circle_point(phase_index, length)
    cosine = cosine * factor
    sine_part = -sine * factor
    return jnp.concatenate([cosine, sine_part], 1).astype(jnp.bfloat16)


def circle_point(phase_index, length):
    quarter_bits = (length // 4).bit_length() - 1
    shifted_index = phase_index + length // 8
    nearest = shifted_index >> quarter_bits
    rest = (shifted_index & (length // 4 - 1)) - length // 8
    x = rest.astype(jnp.float32) * (two_pi / length)
    x2 = x * x
    sin_x = x * (1.0 + x2 * (-1.0 / 6.0 + x2 * (1.0 / 120.0 + x2 * (-1.0 / 5040.0))))
    cos_x = 1.0 + x2 * (-0.5 + x2 * (1.0 / 24.0 + x2 * (-1.0 / 720.0 + x2 * (1.0 / 40320.0))))
    swap = (nearest & 1) == 1
    sine = jnp.where(swap, cos_x, sin_x)
    cosine = jnp.where(swap, sin_x, cos_x)
    sine = jnp.where((nearest & 2) != 0, -sine, sine)
    cosine = jnp.where(((nearest + 1) & 2) != 0, -cosine, cosine)
    return cosine, sine


def shifted(x, axis, shift):
    count = lax.axis_size(axis)
    return lax.ppermute(x, axis, [(j, (j + shift) % count) for j in range(count)])


def ring_sum(x, axis):
    total = x
    for shift in range(1, lax.axis_size(axis)):
        total = total + shifted(x, axis, shift)
    return total


def gather_stack(x, axis):
    count = lax.axis_size(axis)
    me = lax.axis_index(axis)
    stack = jnp.stack([x] + [shifted(x, axis, shift) for shift in range(1, count)])
    return stack[(me - jnp.arange(count)) % count]


def scatter_sum(x, axis):
    count = lax.axis_size(axis)
    lead = x.shape[:-1]
    parts = x.reshape(lead + (count, x.shape[-1] // count))
    parts = jnp.moveaxis(parts, -2, 0).reshape(count, -1)
    total = jnp.sum(lax.all_to_all(parts, axis, 0, 0, tiled=True), axis=0)
    return total.reshape(lead + (x.shape[-1] // count,))


def gather_last(x, axis):
    count = lax.axis_size(axis)
    copies = jnp.broadcast_to(x.reshape(1, -1), (count, x.size))
    joined = lax.all_to_all(copies, axis, 0, 0, tiled=True).reshape((count,) + x.shape)
    joined = jnp.moveaxis(joined, 0, -2)
    return joined.reshape(x.shape[:-1] + (count * x.shape[-1],))


def on_device(histories, bin_index, delays, map_adjoint):
    groups = lax.axis_size("grp")
    position = lax.axis_index("grp")
    bins = bin_index.shape[0]
    sensors = delays.shape[0] * lax.axis_size(SENS_AXES)
    steer_scale = 1.0 / math.sqrt(sensors)
    samples = histories.shape[1]
    scan_share = delays.shape[1] // groups

    transform = transform_rows(position * samples, samples, bin_index, NT)
    spectra = jnp.dot(histories, transform, preferred_element_type=jnp.float32)
    spectra = ring_sum(spectra, "grp")
    real_t = spectra[:, :bins].T
    imag_t = spectra[:, bins:].T

    own_delays = lax.dynamic_slice_in_dim(delays, position * scan_share, scan_share, 1)
    phase_index = bin_index[:, None, None] * own_delays[None, :, :]
    cosine, sine_part = lax.optimization_barrier(circle_point(phase_index, NT))

    own_weight = (2.0 * steer_scale) * lax.dynamic_slice_in_dim(
        map_adjoint, position * scan_share, scan_share, 0
    )
    steer_real = jnp.sum(real_t[:, :, None] * cosine - imag_t[:, :, None] * sine_part, axis=1)
    steer_imag = jnp.sum(real_t[:, :, None] * sine_part + imag_t[:, :, None] * cosine, axis=1)
    steered = jnp.stack([steer_real, steer_imag]) * own_weight
    offset = 0
    for axis in SENS_AXES:
        offset = offset * lax.axis_size(axis) + lax.axis_index(axis)
    count = lax.axis_size(SENS_AXES)
    parts = steered.reshape(count, steered.size // count)
    width = parts.shape[1]
    moved = lax.all_to_all(parts, SENS_AXES, 0, 0, tiled=True)
    chunk = jnp.sum(moved, axis=0)
    copies = jnp.broadcast_to(chunk[None], (count, width))
    gathered = lax.all_to_all(copies, SENS_AXES, 0, 0, tiled=True).reshape(steered.shape)
    bar = gathered
    bar_real = bar[0]
    bar_imag = bar[1]

    back_real = jnp.sum(bar_real[:, None, :] * cosine + bar_imag[:, None, :] * sine_part, axis=2)
    back_imag = jnp.sum(bar_imag[:, None, :] * cosine - bar_real[:, None, :] * sine_part, axis=2)
    back = jnp.concatenate([back_real.T, back_imag.T], 1) * steer_scale
    back = ring_sum(back, "grp")
    adjoint = back.astype(jnp.bfloat16)
    local_part = lax.dot_general(
        adjoint, transform, (((1,), (1,)), ((), ())), preferred_element_type=jnp.float32
    )
    return local_part.astype(jnp.bfloat16)


SENS_AXES = ("sx", "sz", "sy")


def solution(mesh):
    sens_size = mesh.shape["sens"]
    side = round(sens_size ** (1.0 / 3.0))
    assert side ** 3 == sens_size
    fine = jax.sharding.Mesh(
        mesh.devices.reshape(side, side, side, mesh.shape["grp"]), SENS_AXES + ("grp",)
    )
    placed = (P(SENS_AXES, "grp"), P(), P(SENS_AXES, None), P())
    return jax.shard_map(
        on_device, mesh=fine, in_specs=placed, out_specs=P(SENS_AXES, "grp"), check_vma=False
    )
```

```python
import math

import jax
import jax.numpy as jnp
from jax import lax
from jax.sharding import PartitionSpec as P

NT = 4096

two_pi = 2.0 * math.pi


def transform_rows(first, count, bin_index, length):
    sample_times = first + lax.iota(jnp.int32, count)
    phase_index = sample_times[:, None] * bin_index[None, :]
    factor = 1.0 / math.sqrt(length)
    cosine, sine = circle_point(phase_index, length)
    cosine = cosine * factor
    sine_part = -sine * factor
    return jnp.concatenate([cosine, sine_part], 1).astype(jnp.bfloat16)


def circle_point(phase_index, length):
    quarter_bits = (length // 4).bit_length() - 1
    shifted_index = phase_index + length // 8
    nearest = shifted_index >> quarter_bits
    rest = (shifted_index & (length // 4 - 1)) - length // 8
    step = two_pi / length
    r = rest.astype(jnp.float32)
    r2 = r * r
    s2 = step * step
    sin_x = r * (step + r2 * (-step * s2 / 6.0 + r2 * (step * s2 * s2 / 120.0 + r2 * (-step * s2 ** 3 / 5040.0))))
    cos_x = 1.0 + r2 * (-s2 / 2.0 + r2 * (s2 ** 2 / 24.0 + r2 * (-s2 ** 3 / 720.0 + r2 * (s2 ** 4 / 40320.0))))
    swap = (nearest & 1) == 1
    sine = jnp.where(swap, cos_x, sin_x)
    cosine = jnp.where(swap, sin_x, cos_x)
    sine = jnp.where((nearest & 2) != 0, -sine, sine)
    cosine = jnp.where(((nearest + 1) & 2) != 0, -cosine, cosine)
    return cosine, sine


def shifted(x, axis, shift):
    count = lax.axis_size(axis)
    return lax.ppermute(x, axis, [(j, (j + shift) % count) for j in range(count)])


def ring_sum(x, axis):
    total = x
    for shift in range(1, lax.axis_size(axis)):
        total = total + shifted(x, axis, shift)
    return total


def gather_stack(x, axis):
    count = lax.axis_size(axis)
    me = lax.axis_index(axis)
    stack = jnp.stack([x] + [shifted(x, axis, shift) for shift in range(1, count)])
    return stack[(me - jnp.arange(count)) % count]


def scatter_sum(x, axis):
    count = lax.axis_size(axis)
    lead = x.shape[:-1]
    parts = x.reshape(lead + (count, x.shape[-1] // count))
    parts = jnp.moveaxis(parts, -2, 0).reshape(count, -1)
    total = jnp.sum(lax.all_to_all(parts, axis, 0, 0, tiled=True), axis=0)
    return total.reshape(lead + (x.shape[-1] // count,))


def gather_last(x, axis):
    count = lax.axis_size(axis)
    copies = jnp.broadcast_to(x.reshape(1, -1), (count, x.size))
    joined = lax.all_to_all(copies, axis, 0, 0, tiled=True).reshape((count,) + x.shape)
    joined = jnp.moveaxis(joined, 0, -2)
    return joined.reshape(x.shape[:-1] + (count * x.shape[-1],))


def on_device(histories, bin_index, delays, map_adjoint):
    groups = lax.axis_size("grp")
    position = lax.axis_index("grp")
    bins = bin_index.shape[0]
    sensors = delays.shape[0] * lax.axis_size(SENS_AXES)
    steer_scale = 1.0 / math.sqrt(sensors)
    samples = histories.shape[1]
    scan_share = delays.shape[1] // groups

    transform = transform_rows(position * samples, samples, bin_index, NT)
    spectra = jnp.dot(histories, transform, preferred_element_type=jnp.float32)
    spectra = ring_sum(spectra, "grp")
    real_t = spectra[:, :bins].T
    imag_t = spectra[:, bins:].T

    own_delays = lax.dynamic_slice_in_dim(delays, position * scan_share, scan_share, 1)
    phase_index = bin_index[:, None, None] * own_delays[None, :, :]
    cosine, sine_part = lax.optimization_barrier(circle_point(phase_index, NT))

    steer_real = jnp.sum(real_t[:, :, None] * cosine - imag_t[:, :, None] * sine_part, axis=1)
    steer_imag = jnp.sum(real_t[:, :, None] * sine_part + imag_t[:, :, None] * cosine, axis=1)
    steered = jnp.stack([steer_real, steer_imag])
    offset = 0
    for axis in SENS_AXES:
        offset = offset * lax.axis_size(axis) + lax.axis_index(axis)
    count = lax.axis_size(SENS_AXES)
    parts = steered.reshape(count, steered.size // count)
    width = parts.shape[1]
    own_weight = (2.0 * steer_scale) * lax.dynamic_slice_in_dim(
        map_adjoint, position * scan_share, scan_share, 0
    )
    parts, own_weight = lax.optimization_barrier((parts, own_weight))
    moved = lax.all_to_all(parts, SENS_AXES, 0, 0, tiled=True)
    chunk = jnp.sum(moved, axis=0)
    copies = jnp.broadcast_to(chunk[None], (count, width))
    gathered = lax.all_to_all(copies, SENS_AXES, 0, 0, tiled=True).reshape(steered.shape)
    bar = own_weight * gathered
    bar_real = bar[0]
    bar_imag = bar[1]

    back_real = jnp.sum(bar_real[:, None, :] * cosine + bar_imag[:, None, :] * sine_part, axis=2)
    back_imag = jnp.sum(bar_imag[:, None, :] * cosine - bar_real[:, None, :] * sine_part, axis=2)
    back = jnp.concatenate([back_real.T, back_imag.T], 1) * steer_scale
    back = ring_sum(back, "grp")
    adjoint = back.astype(jnp.bfloat16)
    local_part = lax.dot_general(
        adjoint, transform, (((1,), (1,)), ((), ())), preferred_element_type=jnp.float32
    )
    return local_part.astype(jnp.bfloat16)


SENS_AXES = ("sx", "sz", "sy")


def solution(mesh):
    sens_size = mesh.shape["sens"]
    side = round(sens_size ** (1.0 / 3.0))
    assert side ** 3 == sens_size
    fine = jax.sharding.Mesh(
        mesh.devices.reshape(side, side, side, mesh.shape["grp"]), SENS_AXES + ("grp",)
    )
    placed = (P(SENS_AXES, "grp"), P(), P(SENS_AXES, None), P())
    return jax.shard_map(
        on_device, mesh=fine, in_specs=placed, out_specs=P(SENS_AXES, "grp"), check_vma=False
    )
```

```python
import math

import jax
import jax.numpy as jnp
from jax import lax
from jax.sharding import PartitionSpec as P

NT = 4096

two_pi = 2.0 * math.pi


def transform_rows(first, count, bin_index, length):
    sample_times = first + lax.iota(jnp.int32, count)
    phase_index = sample_times[:, None] * bin_index[None, :]
    factor = 1.0 / math.sqrt(length)
    cosine, sine = circle_point(phase_index, length)
    cosine = cosine * factor
    sine_part = -sine * factor
    return jnp.concatenate([cosine, sine_part], 1).astype(jnp.bfloat16)


def circle_point(phase_index, length):
    quarter_bits = (length // 4).bit_length() - 1
    shifted_index = phase_index + length // 8
    nearest = shifted_index >> quarter_bits
    rest = (shifted_index & (length // 4 - 1)) - length // 8
    x = rest.astype(jnp.float32) * (two_pi / length)
    x2 = x * x
    sin_x = x * (1.0 + x2 * (-1.0 / 6.0 + x2 * (1.0 / 120.0 + x2 * (-1.0 / 5040.0))))
    cos_x = 1.0 + x2 * (-0.5 + x2 * (1.0 / 24.0 + x2 * (-1.0 / 720.0 + x2 * (1.0 / 40320.0))))
    swap = (nearest & 1) == 1
    sine = jnp.where(swap, cos_x, sin_x)
    cosine = jnp.where(swap, sin_x, cos_x)
    sine = jnp.where((nearest & 2) != 0, -sine, sine)
    cosine = jnp.where(((nearest + 1) & 2) != 0, -cosine, cosine)
    return cosine, sine


def shifted(x, axis, shift):
    count = lax.axis_size(axis)
    return lax.ppermute(x, axis, [(j, (j + shift) % count) for j in range(count)])


def ring_sum(x, axis):
    count = lax.axis_size(axis)
    order = sorted(range(1, count), key=lambda shift: (shift != count // 2, shift))
    total = x
    for shift in order:
        total = total + shifted(x, axis, shift)
    return total


def gather_stack(x, axis):
    count = lax.axis_size(axis)
    me = lax.axis_index(axis)
    stack = jnp.stack([x] + [shifted(x, axis, shift) for shift in range(1, count)])
    return stack[(me - jnp.arange(count)) % count]


def scatter_sum(x, axis):
    count = lax.axis_size(axis)
    lead = x.shape[:-1]
    parts = x.reshape(lead + (count, x.shape[-1] // count))
    parts = jnp.moveaxis(parts, -2, 0).reshape(count, -1)
    total = jnp.sum(lax.all_to_all(parts, axis, 0, 0, tiled=True), axis=0)
    return total.reshape(lead + (x.shape[-1] // count,))


def gather_last(x, axis):
    count = lax.axis_size(axis)
    copies = jnp.broadcast_to(x.reshape(1, -1), (count, x.size))
    joined = lax.all_to_all(copies, axis, 0, 0, tiled=True).reshape((count,) + x.shape)
    joined = jnp.moveaxis(joined, 0, -2)
    return joined.reshape(x.shape[:-1] + (count * x.shape[-1],))


def on_device(histories, bin_index, delays, map_adjoint):
    groups = lax.axis_size("grp")
    position = lax.axis_index("grp")
    bins = bin_index.shape[0]
    sensors = delays.shape[0] * lax.axis_size(SENS_AXES)
    steer_scale = 1.0 / math.sqrt(sensors)
    samples = histories.shape[1]
    scan_share = delays.shape[1] // groups

    transform = transform_rows(position * samples, samples, bin_index, NT)
    spectra = jnp.dot(histories, transform, preferred_element_type=jnp.float32)
    spectra = ring_sum(spectra, "grp")
    real_t = spectra[:, :bins].T
    imag_t = spectra[:, bins:].T

    own_delays = lax.dynamic_slice_in_dim(delays, position * scan_share, scan_share, 1)
    phase_index = bin_index[:, None, None] * own_delays[None, :, :]
    cosine, sine_part = lax.optimization_barrier(circle_point(phase_index, NT))

    steer_real = jnp.sum(real_t[:, :, None] * cosine - imag_t[:, :, None] * sine_part, axis=1)
    steer_imag = jnp.sum(real_t[:, :, None] * sine_part + imag_t[:, :, None] * cosine, axis=1)
    steered = jnp.stack([steer_real, steer_imag])
    offset = 0
    for axis in SENS_AXES:
        offset = offset * lax.axis_size(axis) + lax.axis_index(axis)
    count = lax.axis_size(SENS_AXES)
    parts = steered.reshape(count, steered.size // count)
    width = parts.shape[1]
    own_weight = (2.0 * steer_scale) * lax.dynamic_slice_in_dim(
        map_adjoint, position * scan_share, scan_share, 0
    )
    parts, own_weight = lax.optimization_barrier((parts, own_weight))
    moved = lax.all_to_all(parts, SENS_AXES, 0, 0, tiled=True)
    chunk = jnp.sum(moved, axis=0)
    copies = jnp.broadcast_to(chunk[None], (count, width))
    gathered = lax.all_to_all(copies, SENS_AXES, 0, 0, tiled=True).reshape(steered.shape)
    bar = own_weight * gathered
    bar_real = bar[0]
    bar_imag = bar[1]

    back_real = jnp.sum(bar_real[:, None, :] * cosine + bar_imag[:, None, :] * sine_part, axis=2)
    back_imag = jnp.sum(bar_imag[:, None, :] * cosine - bar_real[:, None, :] * sine_part, axis=2)
    back = jnp.concatenate([back_real.T, back_imag.T], 1) * steer_scale
    back = ring_sum(back, "grp")
    adjoint = back.astype(jnp.bfloat16)
    local_part = lax.dot_general(
        adjoint, transform, (((1,), (1,)), ((), ())), preferred_element_type=jnp.float32
    )
    return local_part.astype(jnp.bfloat16)


SENS_AXES = ("sx", "sz", "sy")


def solution(mesh):
    sens_size = mesh.shape["sens"]
    side = round(sens_size ** (1.0 / 3.0))
    assert side ** 3 == sens_size
    fine = jax.sharding.Mesh(
        mesh.devices.reshape(side, side, side, mesh.shape["grp"]), SENS_AXES + ("grp",)
    )
    placed = (P(SENS_AXES, "grp"), P(), P(SENS_AXES, None), P())
    return jax.shard_map(
        on_device, mesh=fine, in_specs=placed, out_specs=P(SENS_AXES, "grp"), check_vma=False
    )
```

```python
import math

import jax
import jax.numpy as jnp
from jax import lax
from jax.sharding import PartitionSpec as P

NT = 4096

two_pi = 2.0 * math.pi


def transform_rows(first, count, bin_index, length):
    sample_times = first + lax.iota(jnp.int32, count)
    phase_index = sample_times[:, None] * bin_index[None, :]
    factor = 1.0 / math.sqrt(length)
    cosine, sine = circle_point(phase_index, length)
    cosine = cosine * factor
    sine_part = -sine * factor
    return jnp.concatenate([cosine, sine_part], 1).astype(jnp.bfloat16)


def circle_point(phase_index, length):
    quarter_bits = (length // 4).bit_length() - 1
    shifted_index = phase_index + length // 8
    nearest = shifted_index >> quarter_bits
    rest = (shifted_index & (length // 4 - 1)) - length // 8
    x = rest.astype(jnp.float32) * (two_pi / length)
    x2 = x * x
    sin_x = x * (1.0 + x2 * (-1.0 / 6.0 + x2 * (1.0 / 120.0 + x2 * (-1.0 / 5040.0))))
    cos_x = 1.0 + x2 * (-0.5 + x2 * (1.0 / 24.0 + x2 * (-1.0 / 720.0 + x2 * (1.0 / 40320.0))))
    swap = (nearest & 1) == 1
    sine = jnp.where(swap, cos_x, sin_x)
    cosine = jnp.where(swap, sin_x, cos_x)
    sine = jnp.where((nearest & 2) != 0, -sine, sine)
    cosine = jnp.where(((nearest + 1) & 2) != 0, -cosine, cosine)
    return cosine, sine


def shifted(x, axis, shift):
    count = lax.axis_size(axis)
    return lax.ppermute(x, axis, [(j, (j + shift) % count) for j in range(count)])


def ring_sum(x, axis):
    total = x
    for shift in range(1, lax.axis_size(axis)):
        total = total + shifted(x, axis, shift)
    return total


def gather_stack(x, axis):
    count = lax.axis_size(axis)
    me = lax.axis_index(axis)
    stack = jnp.stack([x] + [shifted(x, axis, shift) for shift in range(1, count)])
    return stack[(me - jnp.arange(count)) % count]


def scatter_sum(x, axis):
    count = lax.axis_size(axis)
    lead = x.shape[:-1]
    parts = x.reshape(lead + (count, x.shape[-1] // count))
    parts = jnp.moveaxis(parts, -2, 0).reshape(count, -1)
    total = jnp.sum(lax.all_to_all(parts, axis, 0, 0, tiled=True), axis=0)
    return total.reshape(lead + (x.shape[-1] // count,))


def gather_last(x, axis):
    count = lax.axis_size(axis)
    copies = jnp.broadcast_to(x.reshape(1, -1), (count, x.size))
    joined = lax.all_to_all(copies, axis, 0, 0, tiled=True).reshape((count,) + x.shape)
    joined = jnp.moveaxis(joined, 0, -2)
    return joined.reshape(x.shape[:-1] + (count * x.shape[-1],))


def on_device(histories, bin_index, delays, map_adjoint):
    groups = lax.axis_size("grp")
    position = lax.axis_index("grp")
    bins = bin_index.shape[0]
    sensors = delays.shape[0] * lax.axis_size(SENS_AXES)
    steer_scale = 1.0 / math.sqrt(sensors)
    samples = histories.shape[1]
    scan_share = delays.shape[1] // groups

    transform = transform_rows(position * samples, samples, bin_index, NT)
    spectra = jnp.dot(histories, transform, preferred_element_type=jnp.float32)
    spectra = ring_sum(spectra, "grp")
    real_t = spectra[:, :bins].T
    imag_t = spectra[:, bins:].T

    own_delays = lax.dynamic_slice_in_dim(delays, position * scan_share, scan_share, 1)
    phase_index = bin_index[:, None, None] * own_delays[None, :, :]
    cosine, sine_part = lax.optimization_barrier(circle_point(phase_index, NT))

    steer_real = jnp.sum(real_t[:, :, None] * cosine - imag_t[:, :, None] * sine_part, axis=1)
    steer_imag = jnp.sum(real_t[:, :, None] * sine_part + imag_t[:, :, None] * cosine, axis=1)
    steered = jnp.stack([steer_real, steer_imag])
    offset = 0
    for axis in SENS_AXES:
        offset = offset * lax.axis_size(axis) + lax.axis_index(axis)
    count = lax.axis_size(SENS_AXES)
    parts = steered.reshape(count, steered.size // count)
    width = parts.shape[1]
    own_weight = (2.0 * steer_scale) * lax.dynamic_slice_in_dim(
        map_adjoint, position * scan_share, scan_share, 0
    )
    parts, own_weight = lax.optimization_barrier((parts, own_weight))
    moved = lax.all_to_all(parts, SENS_AXES, 0, 0, tiled=True)
    chunk = jnp.sum(moved, axis=0)
    copies = jnp.broadcast_to(chunk[None], (count, width))
    gathered = lax.all_to_all(copies, SENS_AXES, 0, 0, tiled=True).reshape(steered.shape)
    bar = own_weight * gathered
    bar_real = bar[0]
    bar_imag = bar[1]

    lanes = 128
    grouped = cosine.shape[:2] + (cosine.shape[2] // lanes, lanes)
    first_real = jnp.sum(
        (bar_real[:, None, :] * cosine + bar_imag[:, None, :] * sine_part).reshape(grouped), axis=2
    )
    first_imag = jnp.sum(
        (bar_imag[:, None, :] * cosine - bar_real[:, None, :] * sine_part).reshape(grouped), axis=2
    )
    first_real, first_imag = lax.optimization_barrier((first_real, first_imag))
    back_real = jnp.sum(first_real, axis=2)
    back_imag = jnp.sum(first_imag, axis=2)
    back = jnp.concatenate([back_real.T, back_imag.T], 1) * steer_scale
    back = ring_sum(back, "grp")
    adjoint = back.astype(jnp.bfloat16)
    local_part = lax.dot_general(
        adjoint, transform, (((1,), (1,)), ((), ())), preferred_element_type=jnp.float32
    )
    return local_part.astype(jnp.bfloat16)


SENS_AXES = ("sx", "sz", "sy")


def solution(mesh):
    sens_size = mesh.shape["sens"]
    side = round(sens_size ** (1.0 / 3.0))
    assert side ** 3 == sens_size
    fine = jax.sharding.Mesh(
        mesh.devices.reshape(side, side, side, mesh.shape["grp"]), SENS_AXES + ("grp",)
    )
    placed = (P(SENS_AXES, "grp"), P(), P(SENS_AXES, None), P())
    return jax.shard_map(
        on_device, mesh=fine, in_specs=placed, out_specs=P(SENS_AXES, "grp"), check_vma=False
    )
```

```python
import math

import jax
import jax.numpy as jnp
from jax import lax
from jax.sharding import PartitionSpec as P

NT = 4096

two_pi = 2.0 * math.pi


def transform_rows(first, count, bin_index, length):
    sample_times = first + lax.iota(jnp.int32, count)
    phase_index = sample_times[:, None] * bin_index[None, :]
    factor = 1.0 / math.sqrt(length)
    cosine, sine = circle_point(phase_index, length)
    cosine = cosine * factor
    sine_part = -sine * factor
    return jnp.concatenate([cosine, sine_part], 1).astype(jnp.bfloat16)


def circle_point(phase_index, length):
    quarter_bits = (length // 4).bit_length() - 1
    shifted_index = phase_index + length // 8
    nearest = shifted_index >> quarter_bits
    rest = (shifted_index & (length // 4 - 1)) - length // 8
    x = rest.astype(jnp.float32) * (two_pi / length)
    x2 = x * x
    sin_x = x * (1.0 + x2 * (-1.0 / 6.0 + x2 * (1.0 / 120.0 + x2 * (-1.0 / 5040.0))))
    cos_x = 1.0 + x2 * (-0.5 + x2 * (1.0 / 24.0 + x2 * (-1.0 / 720.0 + x2 * (1.0 / 40320.0))))
    swap = (nearest & 1) == 1
    sine = jnp.where(swap, cos_x, sin_x)
    cosine = jnp.where(swap, sin_x, cos_x)
    sine = jnp.where((nearest & 2) != 0, -sine, sine)
    cosine = jnp.where(((nearest + 1) & 2) != 0, -cosine, cosine)
    return cosine, sine


def shifted(x, axis, shift):
    count = lax.axis_size(axis)
    return lax.ppermute(x, axis, [(j, (j + shift) % count) for j in range(count)])


def ring_sum(x, axis):
    total = x
    for shift in range(1, lax.axis_size(axis)):
        total = total + shifted(x, axis, shift)
    return total


def gather_stack(x, axis):
    count = lax.axis_size(axis)
    me = lax.axis_index(axis)
    stack = jnp.stack([x] + [shifted(x, axis, shift) for shift in range(1, count)])
    return stack[(me - jnp.arange(count)) % count]


def scatter_sum(x, axis):
    count = lax.axis_size(axis)
    lead = x.shape[:-1]
    parts = x.reshape(lead + (count, x.shape[-1] // count))
    parts = jnp.moveaxis(parts, -2, 0).reshape(count, -1)
    total = jnp.sum(lax.all_to_all(parts, axis, 0, 0, tiled=True), axis=0)
    return total.reshape(lead + (x.shape[-1] // count,))


def gather_last(x, axis):
    count = lax.axis_size(axis)
    copies = jnp.broadcast_to(x.reshape(1, -1), (count, x.size))
    joined = lax.all_to_all(copies, axis, 0, 0, tiled=True).reshape((count,) + x.shape)
    joined = jnp.moveaxis(joined, 0, -2)
    return joined.reshape(x.shape[:-1] + (count * x.shape[-1],))


def on_device(histories, bin_index, delays, map_adjoint):
    groups = lax.axis_size("grp")
    position = lax.axis_index("grp")
    bins = bin_index.shape[0]
    sensors = delays.shape[0] * lax.axis_size(SENS_AXES)
    steer_scale = 1.0 / math.sqrt(sensors)
    samples = histories.shape[1]
    scan_share = delays.shape[1] // groups

    transform = transform_rows(position * samples, samples, bin_index, NT)
    spectra = jnp.dot(histories, transform, preferred_element_type=jnp.float32)
    spectra = ring_sum(spectra, "grp")
    real_t = spectra[:, :bins].T
    imag_t = spectra[:, bins:].T

    own_delays = lax.dynamic_slice_in_dim(delays, position * scan_share, scan_share, 1)
    phase_index = bin_index[:, None, None] * own_delays[None, :, :]
    cosine, sine_part = lax.optimization_barrier(circle_point(phase_index, NT))

    steer_real = jnp.sum(real_t[:, :, None] * cosine - imag_t[:, :, None] * sine_part, axis=1)
    steer_imag = jnp.sum(real_t[:, :, None] * sine_part + imag_t[:, :, None] * cosine, axis=1)
    steered = jnp.stack([steer_real, steer_imag])
    offset = 0
    for axis in SENS_AXES:
        offset = offset * lax.axis_size(axis) + lax.axis_index(axis)
    count = lax.axis_size(SENS_AXES)
    parts = steered.reshape(count, steered.size // count)
    width = parts.shape[1]
    own_weight = (2.0 * steer_scale * steer_scale) * lax.dynamic_slice_in_dim(
        map_adjoint, position * scan_share, scan_share, 0
    )
    parts, own_weight = lax.optimization_barrier((parts, own_weight))
    moved = lax.all_to_all(parts, SENS_AXES, 0, 0, tiled=True)
    chunk = jnp.sum(moved, axis=0)
    copies = jnp.broadcast_to(chunk[None], (count, width))
    gathered = lax.all_to_all(copies, SENS_AXES, 0, 0, tiled=True).reshape(steered.shape)
    bar = own_weight * gathered
    bar_real = bar[0]
    bar_imag = bar[1]

    back_real = jnp.sum(bar_real[:, None, :] * cosine + bar_imag[:, None, :] * sine_part, axis=2)
    back_imag = jnp.sum(bar_imag[:, None, :] * cosine - bar_real[:, None, :] * sine_part, axis=2)
    back = jnp.concatenate([back_real.T, back_imag.T], 1)
    back = ring_sum(back, "grp")
    adjoint = back.astype(jnp.bfloat16)
    local_part = lax.dot_general(
        adjoint, transform, (((1,), (1,)), ((), ())), preferred_element_type=jnp.float32
    )
    return local_part.astype(jnp.bfloat16)


SENS_AXES = ("sx", "sz", "sy")


def solution(mesh):
    sens_size = mesh.shape["sens"]
    side = round(sens_size ** (1.0 / 3.0))
    assert side ** 3 == sens_size
    fine = jax.sharding.Mesh(
        mesh.devices.reshape(side, side, side, mesh.shape["grp"]), SENS_AXES + ("grp",)
    )
    placed = (P(SENS_AXES, "grp"), P(), P(SENS_AXES, None), P())
    return jax.shard_map(
        on_device, mesh=fine, in_specs=placed, out_specs=P(SENS_AXES, "grp"), check_vma=False
    )
```
